256 devices in a mesh: tok: 16 (over z, core), tp: 16 (over x, y).
Axes of the slice: x: 4, y: 4, z: 8, core: 2. Of those that a mesh axis runs over, the one named last changes fastest.
Arguments:
- hidden_states: bfloat16 [32768, 1024], P(('tok', 'tp')), may hold values from -40 to 40
- first_gain: float32 [1024], replicated, may hold values from 0.1 to 1.9
- second_gain: float32 [1024], replicated, may hold values from 0.1 to 1.9
- w_query: bfloat16 [1024, 1024], P(None, 'tp'), may hold values from -1 to 1
- w_keyval: bfloat16 [1024, 1024], replicated, may hold values from -0.375 to 0.375
- w_out: bfloat16 [1024, 1024], P('tp'), may hold values from -0.75 to 0.75
- kv_cache: bfloat16 [384, 128, 1024], P('tok'), may hold values from -310 to 310
- page_table: int32 [32, 16], P('tok'), may hold values from 0 to 383, as said below
- cached_len: int32 [32], P('tok'), may hold values from 128 to 2048, as said below
- expert_ids: int32 [32768, 8], P(('tok', 'tp')), may hold values from 0 to 31, all different within a row; in each aligned block of 128 rows (0 to 127, 128 to 255, ...) at most 64 rows name the same one
- gate_weights: float32 [32768, 8], P(('tok', 'tp')), may hold values from 0.1 to 1
- w_gate_up: bfloat16 [32, 1024, 1024], P('tp', 'tok'), may hold values from -0.1875 to 0.1875
- w_down: bfloat16 [32, 512, 1024], P('tp', 'tok'), may hold values from -1 to 1
Outputs:
- layer_out: bfloat16 [32768, 1024], P(('tok', 'tp'))
The draws below stay inside these ranges and needn't reach their ends.
Inputs may be any that keep to these rules, and one draw needn't show every extreme that they name: `page_table`: request r's entries are pages of its own tok index, rows 24 * (r // 2) to 24 * (r // 2 + 1) - 1; its first 8 entries are the same for all requests of that tok index, and all other entries name pages that no other entry names. `cached_len`: some request has exactly 2048 cached tokens. `expert_ids`: in the rows of one device (aligned blocks of 128 rows) no expert is named by more than 64 rows, and a row names 8 different experts.
All inputs are finite; a program needn't handle non-finite values.
Results may differ from the reference program's by a relative error of at most 0.017.
The reference program's roundings to bfloat16 on the way count: a program that leaves them out, or rounds other values in their place, can miss the bound.
Values may be sent and summed in bfloat16 or wider, within the bound.
No kernel may reach another device: no remote copies, remote signals or barrier semaphores. Data moves between devices by JAX's collectives and lax.ppermute only.
A program may use at most 128 MiB of HBM per device.

```python
import math
import jax
import jax.numpy as jnp
import numpy as np
from jax import lax

D = 1024
HEADS = 16
KV_HEADS = 8
HEAD_DIM = 64
EXPERTS = 32
FF_EXPERT = 512
TOP = 8
PAGE = 128
NEW = 1024
MAX_CACHED = 2048
SHARED_PAGES = 8
REQ_DEV = 2
REQUESTS = 32
TOKENS = 32768
TOK_DEV = 128
CAPACITY = 64
MAX_PAGES = 16
POOL_DEV = 24
POOL = 384


def table_pages(key):
    groups = REQUESTS // REQ_DEV
    group_keys = jax.random.split(jax.random.fold_in(key, 7), groups)

    def one_order(group_key):
        return jax.random.permutation(group_key, POOL_DEV)
    orders = jax.vmap(one_order)(group_keys)
    request_ids = jnp.arange(REQUESTS)
    group_of = request_ids // REQ_DEV
    within = request_ids % REQ_DEV
    page_pos = jnp.arange(MAX_PAGES)
    slot_ids = jnp.where(page_pos[None, :] < SHARED_PAGES, page_pos[None, :], SHARED_PAGES + within[:, None] * (MAX_PAGES - SHARED_PAGES) + page_pos[None, :] - SHARED_PAGES)
    return group_of[:, None] * POOL_DEV + orders[group_of[:, None], slot_ids]


def draw_page_table(key, part):
    return table_pages(key).astype(jnp.int32)


def draw_cached_len(key, part):
    lengths = jax.random.randint(jax.random.fold_in(key, 11), (REQUESTS,), PAGE, MAX_CACHED + 1)
    longest = jax.random.randint(jax.random.fold_in(key, 13), (), 0, REQUESTS)
    return jnp.where(jnp.arange(REQUESTS) == longest, MAX_CACHED, lengths).astype(jnp.int32)


def draw_kv_cache(key, part):
    base_key = jax.random.fold_in(jax.random.fold_in(key, 3), 0)
    shape = (POOL, PAGE, 2 * KV_HEADS * HEAD_DIM)
    cache = jax.random.truncated_normal(base_key, -6.0, 6.0, shape, jnp.float32) * 2.0
    return cache.astype(jnp.bfloat16)


def draw_hidden_states(key, part):
    noise_key, row_key, column_key = jax.random.split(jax.random.fold_in(key, 5), 3)
    row_scale = jnp.exp(jax.random.uniform(row_key, (TOKENS, 1), jnp.float32, -1.1513, 1.1513))
    column_scale = jnp.exp(jax.random.uniform(column_key, (1, D), jnp.float32, -1.1513, 1.1513))
    values = jax.random.truncated_normal(noise_key, -4.0, 4.0, (TOKENS, D), jnp.float32)
    return (values * row_scale * column_scale).astype(jnp.bfloat16)


def shard_levels(rng, shape, pieces, low, largest):
    def one(axis_at, parts):
        draws = jax.random.uniform(jax.random.fold_in(jax.random.fold_in(rng, 6), axis_at), (parts,), jnp.float32, low / len(pieces), largest / len(pieces))
        return jnp.repeat(jnp.exp(draws), shape[axis_at] // parts).reshape((-1,) + (1,) * (len(shape) - axis_at - 1))

    level = one(*pieces[0])
    for cut in pieces[1:]:
        level = level * one(*cut)
    return level


def deal_out(stream_key, own, number, rows, count, top, most, lean):
    sequence = jax.random.permutation(stream_key, count)
    crowded, usual = load_shares(count, rows * top, most, lean, True), load_shares(count, rows * top, most, lean, False)
    places = jnp.arange(count)

    def named(sizes, turn):
        used = int((sizes > 0).sum())
        fixed = max(1, used // 4)
        passed = fixed + (places - fixed + turn * (used - fixed)) % max(1, count - fixed)
        return jnp.zeros((count,), jnp.int32).at[sequence[jnp.where(places < fixed, places, passed)]].set(jnp.asarray(sizes, jnp.int32))

    sizes = jnp.where(number % 4 == 0, named(crowded, number // 4), named(usual, number - number // 4 - 1))
    mixed = jax.random.permutation(jax.random.fold_in(own, 3), count)
    giver, taker = mixed[0:count // 2 * 2:2], mixed[1:count // 2 * 2:2]
    margin = jnp.minimum(sizes[giver] - 1, most - sizes[taker]) // 2
    margin = jnp.where((giver == sequence[0]) | (taker == sequence[0]) | (sizes[taker] == 0), 0, jnp.maximum(margin, 0))
    passed = jax.random.randint(jax.random.fold_in(own, 4), (count // 2,), 0, 1 << 20) % (margin + 1)
    sizes = sizes.at[giver].add(-passed).at[taker].add(passed)
    labels = jnp.searchsorted(jnp.cumsum(sizes), jnp.arange(rows * top), side="right").astype(jnp.int32)
    table = labels.reshape(top, rows).T
    table = table[jax.random.permutation(jax.random.fold_in(own, 1), rows)]
    turn = jax.random.randint(jax.random.fold_in(own, 2), (rows, 1), 0, top)
    return jnp.take_along_axis(table, (jnp.arange(top)[None, :] + turn) % top, axis=1)


def load_shares(number_of, total, reach, skew, full):
    portions = [(1 << 20) // math.isqrt(rank ** skew) + 1 for rank in range(1, number_of + 1)]
    largest = reach if full else min(reach, max(-(-total // number_of), total * portions[0] // sum(portions)))
    least = 1 if total - largest >= number_of - 1 else 0
    given, spare = [largest] + [least] * (number_of - 1), total - largest - least * (number_of - 1)
    while spare > 0:
        candidates = [i for i in range(1, number_of) if given[i] < largest] or [i for i in range(1, number_of) if given[i] < reach]
        mass, left = sum([portions[i] for i in candidates]), spare
        for i in candidates:
            more = min(reach - given[i], max(1, left * portions[i] // mass), spare)
            given[i] = given[i] + more
            spare = spare - more
    return np.array(given)


def centred(rng, shape, deviation, limit, pieces=(), held_as=jnp.bfloat16):
    result = jax.random.normal(rng, shape, jnp.float32) * deviation
    if len(pieces) > 0:
        result = shard_levels(rng, shape, pieces, -0.22, 0.18) * result
    return jnp.clip(result, min=-limit, max=limit).astype(held_as)


def setup_inputs(seed: int = 0) -> dict:
    key_list = jax.random.split(jax.random.key(seed), 14)
    hidden_states = draw_hidden_states(jax.random.fold_in(key_list[13], 71), 0)
    first_gain = jnp.clip(1.0 + 0.18 * jax.random.normal(key_list[1], (D,), jnp.float32), 0.1, 1.9)
    second_gain = jnp.clip(1.0 + 0.18 * jax.random.normal(key_list[2], (D,), jnp.float32), 0.1, 1.9)
    w_query = centred(key_list[3], (D, HEADS * HEAD_DIM), (D // 32) ** -0.5, 1.0, ((1, 16),))
    w_keyval = centred(key_list[4], (D, 2 * KV_HEADS * HEAD_DIM), (D // 4) ** -0.5, 0.375)
    w_out = centred(key_list[5], (HEADS * HEAD_DIM, D), (HEADS * HEAD_DIM // 16) ** -0.5, 0.75, ((0, 16),))
    kv_cache = draw_kv_cache(jax.random.fold_in(key_list[13], 71), 0)
    page_table = draw_page_table(jax.random.fold_in(key_list[13], 71), 0)
    cached_len = draw_cached_len(jax.random.fold_in(key_list[13], 71), 0)
    expert_ids_keys = jax.random.split(jax.random.fold_in(key_list[9], 1), TOKENS // TOK_DEV)
    expert_ids_turns = jax.random.permutation(jax.random.fold_in(key_list[9], 3), TOKENS // TOK_DEV)
    expert_ids = jax.vmap(lambda own, number: deal_out(jax.random.fold_in(key_list[9], 2), own, number, TOK_DEV, EXPERTS, TOP, CAPACITY, 2))(expert_ids_keys, expert_ids_turns).reshape((TOKENS, TOP))
    gate_weights = jnp.clip(jnp.exp(math.log(1.0) - 2.3025851 * jax.random.uniform(key_list[10], (TOKENS, TOP), jnp.float32) ** shard_levels(key_list[10], (TOKENS, TOP), ((0, 256),), -0.2, 0.2)), 0.1, 1.0)
    w_gate_up = centred(key_list[11], (EXPERTS, D, 2 * FF_EXPERT), D ** -0.5, 0.1875, ((0, 16), (1, 16)))
    w_down = centred(key_list[12], (EXPERTS, FF_EXPERT, D), (FF_EXPERT // 16) ** -0.5, 1.0, ((0, 16), (1, 16)))
    return {"hidden_states": hidden_states, "first_gain": first_gain, "second_gain": second_gain, "w_query": w_query, "w_keyval": w_keyval, "w_out": w_out, "kv_cache": kv_cache, "page_table": page_table, "cached_len": cached_len, "expert_ids": expert_ids, "gate_weights": gate_weights, "w_gate_up": w_gate_up, "w_down": w_down}


ATTN_SCALE = 0.015625
EPSILON = 1e-06
THETA = 10000.0

def rms_norm(values, gain):
    wide = values.astype(jnp.float32)
    factor = lax.rsqrt(lax.optimization_barrier(jnp.mean(wide * wide, axis=-1, keepdims=True)) + EPSILON)
    return (wide * factor * gain).astype(jnp.bfloat16)

def rotate(values, positions):
    row_count = values.shape[0]
    shaped = values.reshape(row_count, -1, HEAD_DIM)
    half_dim = HEAD_DIM // 2
    exponent = jnp.arange(half_dim).astype(jnp.float32) * (2.0 / HEAD_DIM)
    frequency = jnp.power(THETA, -exponent)
    angles = positions.astype(jnp.float32)[:, None] * frequency[None, :]
    cosine = jnp.cos(angles)[:, None, :]
    sine_part = jnp.sin(angles)[:, None, :]
    leading = shaped[..., :half_dim]
    trailing = shaped[..., half_dim:]
    turned = jnp.concatenate([leading * cosine - trailing * sine_part, trailing * cosine + leading * sine_part], axis=-1)
    return turned.reshape(row_count, -1)

def attend_request(queries, keys_total, values_total, length):
    block_rows = min(NEW, 512)
    key_index = jnp.arange(MAX_CACHED + NEW).astype(jnp.int32)
    keys_wide = keys_total.astype(jnp.float32)
    values_wide = values_total.astype(jnp.float32)

    def one_block(block_start):
        block_query = lax.dynamic_slice_in_dim(queries, block_start, block_rows, 0).astype(jnp.float32)
        scores = jnp.einsum('qgpd,kgd->gpqk', block_query, keys_wide) * ATTN_SCALE
        query_pos = block_start + jnp.arange(block_rows).astype(jnp.int32)
        allowed = jnp.where(key_index[None, :] < MAX_CACHED, key_index[None, :] < length, key_index[None, :] - MAX_CACHED <= query_pos[:, None])
        scores = jnp.where(allowed, scores, -1e+30)
        top_score = lax.optimization_barrier(jnp.max(scores, axis=-1, keepdims=True))
        weights = jnp.exp(scores - top_score)
        probs = (weights / lax.optimization_barrier(jnp.sum(weights, axis=-1, keepdims=True))).astype(jnp.bfloat16)
        mixed = jnp.einsum('gpqk,kgd->qgpd', probs.astype(jnp.float32), values_wide)
        return mixed.astype(jnp.bfloat16).reshape(block_rows, -1)
    starts = jnp.arange(NEW // block_rows).astype(jnp.int32) * block_rows
    return lax.map(one_block, starts).reshape(NEW, -1)

def reference(hidden_states, first_gain, second_gain, w_query, w_keyval, w_out, kv_cache, page_table, cached_len, expert_ids, gate_weights, w_gate_up, w_down):
    group_size = HEADS // KV_HEADS
    kv_cols = KV_HEADS * HEAD_DIM
    normed = rms_norm(hidden_states, first_gain)
    positions = (cached_len[:, None] + jnp.arange(NEW).astype(jnp.int32)[None, :]).reshape(-1)
    queries = rotate(jnp.dot(normed, w_query, preferred_element_type=jnp.float32), positions).astype(jnp.bfloat16)
    keyval = jnp.dot(normed, w_keyval, preferred_element_type=jnp.float32)
    new_keys = rotate(keyval[:, :kv_cols], positions).astype(jnp.bfloat16)
    new_values = keyval[:, kv_cols:].astype(jnp.bfloat16)

    def per_request(inputs):
        page_ids, length, request_q, request_k, request_v = inputs
        cached = kv_cache[page_ids].reshape(MAX_CACHED, 2 * kv_cols)
        keys_total = jnp.concatenate([cached[:, :kv_cols], request_k], axis=0).reshape(MAX_CACHED + NEW, KV_HEADS, HEAD_DIM)
        values_total = jnp.concatenate([cached[:, kv_cols:], request_v], axis=0).reshape(MAX_CACHED + NEW, KV_HEADS, HEAD_DIM)
        return attend_request(request_q.reshape(NEW, KV_HEADS, group_size, HEAD_DIM), keys_total, values_total, length)
    attended = lax.map(per_request, (page_table, cached_len, queries.reshape(REQUESTS, NEW, -1), new_keys.reshape(REQUESTS, NEW, -1), new_values.reshape(REQUESTS, NEW, -1)))
    attended = attended.reshape(TOKENS, HEADS * HEAD_DIM)
    projected = jnp.dot(attended, w_out, preferred_element_type=jnp.float32)
    middle = (hidden_states.astype(jnp.float32) + projected).astype(jnp.bfloat16)
    normed_two = rms_norm(middle, second_gain)
    bound = TOKENS // TOK_DEV * CAPACITY

    def per_expert(accum, expert):
        chosen = expert_ids == expert
        picked = jnp.any(chosen, axis=1)
        weight_row = lax.optimization_barrier(jnp.sum(jnp.where(chosen, gate_weights, 0.0), axis=1))
        row_ids = jnp.nonzero(picked, size=bound, fill_value=0)[0]
        valid = jnp.arange(bound) < jnp.sum(picked)
        rows_in = normed_two[row_ids]
        both = jnp.dot(rows_in, w_gate_up[expert], preferred_element_type=jnp.float32)
        activated = (jax.nn.silu(both[:, :FF_EXPERT]) * both[:, FF_EXPERT:]).astype(jnp.bfloat16)
        produced = jnp.dot(activated, w_down[expert], preferred_element_type=jnp.float32).astype(jnp.bfloat16)
        scaled = jnp.where(valid[:, None], weight_row[row_ids][:, None] * produced.astype(jnp.float32), 0.0)
        return (accum.at[row_ids].add(scaled), None)
    accum, unused = lax.scan(per_expert, jnp.zeros((TOKENS, D), jnp.float32), jnp.arange(EXPERTS).astype(jnp.int32))
    return (middle.astype(jnp.float32) + accum).astype(jnp.bfloat16)
```

```python
import jax
import jax.numpy as jnp
from jax import lax
from jax.sharding import Mesh
from jax.sharding import PartitionSpec as P

D = 1024
HEADS = 16
KV_HEADS = 8
HEAD_DIM = 64
EXPERTS = 32
FF_EXPERT = 512
TOP = 8
NEW = 1024
MAX_CACHED = 2048
REQ_DEV = 2


ATTN_SCALE = 0.015625
EPSILON = 1e-06
THETA = 10000.0

TOK = ("tz", "tc")
TP = ("ra", "rb")


def rms_norm(values, gain):
    wide = values.astype(jnp.float32)
    factor = lax.rsqrt(jnp.mean(wide * wide, axis=-1, keepdims=True) + EPSILON)
    return (wide * factor * gain).astype(jnp.bfloat16)


def rotate(values, positions):
    row_count = values.shape[0]
    shaped = values.reshape(row_count, -1, HEAD_DIM)
    half_dim = HEAD_DIM // 2
    exponent = jnp.arange(half_dim).astype(jnp.float32) * (2.0 / HEAD_DIM)
    frequency = jnp.power(THETA, -exponent)
    angles = positions.astype(jnp.float32)[:, None] * frequency[None, :]
    cosine = jnp.cos(angles)[:, None, :]
    sine_part = jnp.sin(angles)[:, None, :]
    leading = shaped[..., :half_dim]
    trailing = shaped[..., half_dim:]
    turned = jnp.concatenate(
        [leading * cosine - trailing * sine_part, trailing * cosine + leading * sine_part], axis=-1
    )
    return turned.reshape(row_count, -1)


def shards(
    hidden_states,
    first_gain,
    second_gain,
    w_query,
    w_keyval,
    w_out,
    kv_cache,
    page_table,
    cached_len,
    expert_ids,
    gate_weights,
    w_gate_up,
    w_down,
):
    tok_rows = hidden_states.shape[0]
    tp_size = lax.axis_size(TP)
    core = lax.axis_index("tc")
    local_req = lax.axis_index("ra")
    block = lax.axis_index("rb")
    kv_cols = KV_HEADS * HEAD_DIM
    group_size = HEADS // KV_HEADS

    half_rows = D // 2
    wq_half = lax.dynamic_slice_in_dim(w_query, core * half_rows, half_rows, 0)
    wq_full = lax.all_gather(
        lax.all_gather(wq_half, TP, axis=1, tiled=True), "tc", axis=0, tiled=True
    )
    wo_half = lax.dynamic_slice_in_dim(w_out, core * half_rows, half_rows, 1)
    wo_full = lax.all_gather(
        lax.all_gather(wo_half, TP, axis=0, tiled=True), "tc", axis=1, tiled=True
    )
    gate_up_full = lax.all_gather(w_gate_up, TOK, axis=1, tiled=True)
    down_full = lax.all_gather(w_down, TOK, axis=1, tiled=True)

    normed = rms_norm(hidden_states, first_gain)
    length = cached_len[local_req]
    positions = length + block * tok_rows + jnp.arange(tok_rows, dtype=jnp.int32)
    keyval = jnp.dot(normed, w_keyval, preferred_element_type=jnp.float32)
    new_kv = jnp.concatenate(
        [rotate(keyval[:, :kv_cols], positions), keyval[:, kv_cols:]], axis=1
    ).astype(jnp.bfloat16)
    request_kv = lax.all_gather(new_kv, "rb", axis=0, tiled=True)
    queries = rotate(
        jnp.dot(normed, wq_full, preferred_element_type=jnp.float32), positions
    ).astype(jnp.bfloat16)

    local_pages = page_table[local_req] - lax.axis_index(TOK) * kv_cache.shape[0]
    cached = jnp.take(kv_cache, local_pages, axis=0).reshape(MAX_CACHED, 2 * kv_cols)
    keys_total = jnp.concatenate([cached[:, :kv_cols], request_kv[:, :kv_cols]], axis=0).reshape(
        MAX_CACHED + NEW, KV_HEADS, HEAD_DIM
    )
    values_total = jnp.concatenate(
        [cached[:, kv_cols:], request_kv[:, kv_cols:]], axis=0
    ).reshape(MAX_CACHED + NEW, KV_HEADS, HEAD_DIM)
    grouped_q = queries.reshape(tok_rows, KV_HEADS, group_size, HEAD_DIM)
    scores = (
        jnp.einsum("qgpd,kgd->gpqk", grouped_q, keys_total, preferred_element_type=jnp.float32)
        * ATTN_SCALE
    )
    key_index = jnp.arange(MAX_CACHED + NEW, dtype=jnp.int32)
    query_pos = block * tok_rows + jnp.arange(tok_rows, dtype=jnp.int32)
    allowed = jnp.where(
        key_index[None, :] < MAX_CACHED,
        key_index[None, :] < length,
        key_index[None, :] - MAX_CACHED <= query_pos[:, None],
    )
    scores = jnp.where(allowed, scores, -1e30)
    top_score = jnp.max(scores, axis=-1, keepdims=True)
    weights = jnp.exp(scores - top_score)
    probs = (weights / jnp.sum(weights, axis=-1, keepdims=True)).astype(jnp.bfloat16)
    attended = (
        jnp.einsum("gpqk,kgd->qgpd", probs, values_total, preferred_element_type=jnp.float32)
        .astype(jnp.bfloat16)
        .reshape(tok_rows, HEADS * HEAD_DIM)
    )
    projected_out = jnp.dot(attended, wo_full, preferred_element_type=jnp.float32)
    middle = (hidden_states.astype(jnp.float32) + projected_out).astype(jnp.bfloat16)
    normed_two = rms_norm(middle, second_gain)

    experts_local = EXPERTS // tp_size
    capacity = 2 * tok_rows * TOP // EXPERTS
    expert_range = jnp.arange(EXPERTS, dtype=jnp.int32)
    onehot = (expert_ids[:, :, None] == expert_range[None, None, :]).astype(jnp.int32)
    per_token = jnp.sum(onehot, axis=1)
    earlier = jnp.cumsum(per_token, axis=0) - per_token
    slot_ids = jnp.sum(onehot * earlier[:, None, :], axis=2)
    target = expert_ids * capacity + slot_ids
    outgoing_rows = jnp.broadcast_to(normed_two[:, None, :], (tok_rows, TOP, D))
    send_buffer = jnp.zeros((EXPERTS * capacity, D), jnp.bfloat16).at[target].set(outgoing_rows)
    received = lax.all_to_all(
        send_buffer.reshape(tp_size, experts_local, capacity, D),
        TP,
        split_axis=0,
        concat_axis=2,
        tiled=True,
    )
    received = received.reshape(experts_local, tp_size * capacity, D)
    both = jnp.einsum("esd,edf->esf", received, gate_up_full, preferred_element_type=jnp.float32)
    activated = (jax.nn.silu(both[..., :FF_EXPERT]) * both[..., FF_EXPERT:]).astype(jnp.bfloat16)
    produced = jnp.einsum(
        "esf,efd->esd", activated, down_full, preferred_element_type=jnp.float32
    ).astype(jnp.bfloat16)
    returned = lax.all_to_all(
        produced.reshape(experts_local, tp_size, capacity, D),
        TP,
        split_axis=1,
        concat_axis=0,
        tiled=True,
    )
    returned = returned.reshape(EXPERTS * capacity, D)
    picked = returned[target]
    mixture = jnp.einsum("tk,tkd->td", gate_weights, picked.astype(jnp.float32))
    return (middle.astype(jnp.float32) + mixture).astype(jnp.bfloat16)


def solution(mesh):
    tok_size, tp_size = mesh.devices.shape
    group = tp_size // REQ_DEV
    split = Mesh(mesh.devices.reshape(tok_size // 2, 2, REQ_DEV, group), TOK + TP)
    in_specs = (
        P(TOK + TP, None),
        P(),
        P(),
        P(None, TP),
        P(),
        P(TP, None),
        P(TOK, None, None),
        P(TOK, None),
        P(TOK),
        P(TOK + TP, None),
        P(TOK + TP, None),
        P(TP, TOK, None),
        P(TP, TOK, None),
    )
    out_specs = P(TOK + TP, None)
    return jax.shard_map(shards, mesh=split, in_specs=in_specs, out_specs=out_specs, check_vma=False)
```

```python
import jax
import jax.numpy as jnp
from jax import lax
from jax.sharding import Mesh
from jax.sharding import PartitionSpec as P

D = 1024
HEADS = 16
KV_HEADS = 8
HEAD_DIM = 64
EXPERTS = 32
FF_EXPERT = 512
TOP = 8
NEW = 1024
MAX_CACHED = 2048
REQ_DEV = 2


ATTN_SCALE = 0.015625
EPSILON = 1e-06
THETA = 10000.0

TOK = ("tz", "tc")
TP = ("ra", "rb")


def rms_norm(values, gain):
    wide = values.astype(jnp.float32)
    factor = lax.rsqrt(jnp.mean(wide * wide, axis=-1, keepdims=True) + EPSILON)
    return (wide * factor * gain).astype(jnp.bfloat16)


def rotate(values, positions):
    row_count = values.shape[0]
    shaped = values.reshape(row_count, -1, HEAD_DIM)
    half_dim = HEAD_DIM // 2
    exponent = jnp.arange(half_dim).astype(jnp.float32) * (2.0 / HEAD_DIM)
    frequency = jnp.power(THETA, -exponent)
    angles = positions.astype(jnp.float32)[:, None] * frequency[None, :]
    cosine = jnp.cos(angles)[:, None, :]
    sine_part = jnp.sin(angles)[:, None, :]
    leading = shaped[..., :half_dim]
    trailing = shaped[..., half_dim:]
    turned = jnp.concatenate(
        [leading * cosine - trailing * sine_part, trailing * cosine + leading * sine_part], axis=-1
    )
    return turned.reshape(row_count, -1)


def gather_rows(piece, axis_name, count):
    send = jnp.broadcast_to(piece[None], (count,) + piece.shape)
    return lax.all_to_all(send, axis_name, split_axis=0, concat_axis=0, tiled=True)


def shards(
    hidden_states,
    first_gain,
    second_gain,
    w_query,
    w_keyval,
    w_out,
    kv_cache,
    page_table,
    cached_len,
    expert_ids,
    gate_weights,
    w_gate_up,
    w_down,
):
    tok_rows = hidden_states.shape[0]
    tp_size = lax.axis_size(TP)
    core = lax.axis_index("tc")
    local_req = lax.axis_index("ra")
    block = lax.axis_index("rb")
    kv_cols = KV_HEADS * HEAD_DIM
    group_size = HEADS // KV_HEADS

    half_rows = D // 2
    wq_half = lax.dynamic_slice_in_dim(w_query, core * half_rows, half_rows, 0)
    wo_half = lax.dynamic_slice_in_dim(w_out, core * half_rows, half_rows, 1)
    pieces = gather_rows(
        jnp.concatenate([wq_half.reshape(-1), wo_half.reshape(-1)]), TP, tp_size
    )
    q_size = wq_half.size
    wq_mine = jnp.transpose(
        pieces[:, :q_size].reshape(tp_size, half_rows, HEAD_DIM), (1, 0, 2)
    ).reshape(half_rows, D)
    wo_mine = pieces[:, q_size:].reshape(D, half_rows)
    wq_other, wo_other = lax.ppermute((wq_mine, wo_mine), "tc", [(0, 1), (1, 0)])
    first = core == 0
    wq_full = jnp.concatenate(
        [jnp.where(first, wq_mine, wq_other), jnp.where(first, wq_other, wq_mine)], axis=0
    )
    wo_full = jnp.concatenate(
        [jnp.where(first, wo_mine, wo_other), jnp.where(first, wo_other, wo_mine)], axis=1
    )
    gate_up_full = lax.all_gather(w_gate_up, TOK, axis=1, tiled=True)
    down_full = lax.all_gather(w_down, TOK, axis=1, tiled=True)

    normed = rms_norm(hidden_states, first_gain)
    length = cached_len[local_req]
    positions = length + block * tok_rows + jnp.arange(tok_rows, dtype=jnp.int32)
    keyval = jnp.dot(normed, w_keyval, preferred_element_type=jnp.float32)
    new_kv = jnp.concatenate(
        [rotate(keyval[:, :kv_cols], positions), keyval[:, kv_cols:]], axis=1
    ).astype(jnp.bfloat16)
    request_kv = gather_rows(new_kv, "rb", lax.axis_size("rb")).reshape(NEW, 2 * kv_cols)
    queries = rotate(
        jnp.dot(normed, wq_full, preferred_element_type=jnp.float32), positions
    ).astype(jnp.bfloat16)

    local_pages = page_table[local_req] - lax.axis_index(TOK) * kv_cache.shape[0]
    cached = jnp.take(kv_cache, local_pages, axis=0).reshape(MAX_CACHED, 2 * kv_cols)
    keys_total = jnp.concatenate([cached[:, :kv_cols], request_kv[:, :kv_cols]], axis=0).reshape(
        MAX_CACHED + NEW, KV_HEADS, HEAD_DIM
    )
    values_total = jnp.concatenate(
        [cached[:, kv_cols:], request_kv[:, kv_cols:]], axis=0
    ).reshape(MAX_CACHED + NEW, KV_HEADS, HEAD_DIM)
    grouped_q = queries.reshape(tok_rows, KV_HEADS, group_size, HEAD_DIM)
    scores = (
        jnp.einsum("qgpd,kgd->gpqk", grouped_q, keys_total, preferred_element_type=jnp.float32)
        * ATTN_SCALE
    )
    key_index = jnp.arange(MAX_CACHED + NEW, dtype=jnp.int32)
    query_pos = block * tok_rows + jnp.arange(tok_rows, dtype=jnp.int32)
    allowed = jnp.where(
        key_index[None, :] < MAX_CACHED,
        key_index[None, :] < length,
        key_index[None, :] - MAX_CACHED <= query_pos[:, None],
    )
    scores = jnp.where(allowed, scores, -1e30)
    top_score = jnp.max(scores, axis=-1, keepdims=True)
    weights = jnp.exp(scores - top_score)
    probs = (weights / jnp.sum(weights, axis=-1, keepdims=True)).astype(jnp.bfloat16)
    attended = (
        jnp.einsum("gpqk,kgd->qgpd", probs, values_total, preferred_element_type=jnp.float32)
        .astype(jnp.bfloat16)
        .reshape(tok_rows, HEADS * HEAD_DIM)
    )
    projected_out = jnp.dot(attended, wo_full, preferred_element_type=jnp.float32)
    middle = (hidden_states.astype(jnp.float32) + projected_out).astype(jnp.bfloat16)
    normed_two = rms_norm(middle, second_gain)

    experts_local = EXPERTS // tp_size
    capacity = 2 * tok_rows * TOP // EXPERTS
    expert_range = jnp.arange(EXPERTS, dtype=jnp.int32)
    onehot = (expert_ids[:, :, None] == expert_range[None, None, :]).astype(jnp.int32)
    per_token = jnp.sum(onehot, axis=1)
    earlier = jnp.cumsum(per_token, axis=0) - per_token
    slot_ids = jnp.sum(onehot * earlier[:, None, :], axis=2)
    target = expert_ids * capacity + slot_ids
    outgoing_rows = jnp.broadcast_to(normed_two[:, None, :], (tok_rows, TOP, D))
    send_buffer = jnp.zeros((EXPERTS * capacity, D), jnp.bfloat16).at[target].set(outgoing_rows)
    received = lax.all_to_all(
        send_buffer.reshape(tp_size, experts_local, capacity, D),
        TP,
        split_axis=0,
        concat_axis=2,
        tiled=True,
    )
    received = received.reshape(experts_local, tp_size * capacity, D)
    both = jnp.einsum("esd,edf->esf", received, gate_up_full, preferred_element_type=jnp.float32)
    activated = (jax.nn.silu(both[..., :FF_EXPERT]) * both[..., FF_EXPERT:]).astype(jnp.bfloat16)
    produced = jnp.einsum(
        "esf,efd->esd", activated, down_full, preferred_element_type=jnp.float32
    ).astype(jnp.bfloat16)
    returned = lax.all_to_all(
        produced.reshape(experts_local, tp_size, capacity, D),
        TP,
        split_axis=1,
        concat_axis=0,
        tiled=True,
    )
    returned = returned.reshape(EXPERTS * capacity, D)
    picked = returned[target]
    mixture = jnp.einsum("tk,tkd->td", gate_weights, picked.astype(jnp.float32))
    return (middle.astype(jnp.float32) + mixture).astype(jnp.bfloat16)


def solution(mesh):
    tok_size, tp_size = mesh.devices.shape
    group = tp_size // REQ_DEV
    split = Mesh(mesh.devices.reshape(tok_size // 2, 2, REQ_DEV, group), TOK + TP)
    in_specs = (
        P(TOK + TP, None),
        P(),
        P(),
        P(None, TP),
        P(),
        P(TP, None),
        P(TOK, None, None),
        P(TOK, None),
        P(TOK),
        P(TOK + TP, None),
        P(TOK + TP, None),
        P(TP, TOK, None),
        P(TP, TOK, None),
    )
    out_specs = P(TOK + TP, None)
    return jax.shard_map(shards, mesh=split, in_specs=in_specs, out_specs=out_specs, check_vma=False)
```

```python
import jax
import jax.numpy as jnp
from jax import lax
from jax.sharding import Mesh
from jax.sharding import PartitionSpec as P

D = 1024
HEADS = 16
KV_HEADS = 8
HEAD_DIM = 64
EXPERTS = 32
FF_EXPERT = 512
TOP = 8
NEW = 1024
MAX_CACHED = 2048
REQ_DEV = 2


ATTN_SCALE = 0.015625
EPSILON = 1e-06
THETA = 10000.0

TOK = ("tz", "tc")
TP = ("ra", "rb")


def rms_norm(values, gain):
    wide = values.astype(jnp.float32)
    factor = lax.rsqrt(jnp.mean(wide * wide, axis=-1, keepdims=True) + EPSILON)
    return (wide * factor * gain).astype(jnp.bfloat16)


def rotate(values, positions):
    row_count = values.shape[0]
    shaped = values.reshape(row_count, -1, HEAD_DIM)
    half_dim = HEAD_DIM // 2
    exponent = jnp.arange(half_dim).astype(jnp.float32) * (2.0 / HEAD_DIM)
    frequency = jnp.power(THETA, -exponent)
    angles = positions.astype(jnp.float32)[:, None] * frequency[None, :]
    cosine = jnp.cos(angles)[:, None, :]
    sine_part = jnp.sin(angles)[:, None, :]
    leading = shaped[..., :half_dim]
    trailing = shaped[..., half_dim:]
    turned = jnp.concatenate(
        [leading * cosine - trailing * sine_part, trailing * cosine + leading * sine_part], axis=-1
    )
    return turned.reshape(row_count, -1)


def gather_rows(piece, axis_name, count):
    send = jnp.broadcast_to(piece[None], (count,) + piece.shape)
    return lax.all_to_all(send, axis_name, split_axis=0, concat_axis=0, tiled=True)


def shards(
    hidden_states,
    first_gain,
    second_gain,
    w_query,
    w_keyval,
    w_out,
    kv_cache,
    page_table,
    cached_len,
    expert_ids,
    gate_weights,
    w_gate_up,
    w_down,
):
    tok_rows = hidden_states.shape[0]
    tp_size = lax.axis_size(TP)
    core = lax.axis_index("tc")
    local_req = lax.axis_index("ra")
    block = lax.axis_index("rb")
    kv_cols = KV_HEADS * HEAD_DIM
    group_size = HEADS // KV_HEADS

    half_rows = D // 2
    wq_half = lax.dynamic_slice_in_dim(w_query, core * half_rows, half_rows, 0)
    wo_half = lax.dynamic_slice_in_dim(w_out, core * half_rows, half_rows, 1)
    lanes = 128
    pieces = gather_rows(
        jnp.concatenate([wq_half.reshape(-1, lanes), wo_half.reshape(-1, lanes)], axis=0),
        TP,
        tp_size,
    )
    q_rows = wq_half.size // lanes
    wq_mine = jnp.transpose(
        pieces[:, :q_rows].reshape(tp_size, half_rows, HEAD_DIM), (1, 0, 2)
    ).reshape(half_rows, D)
    wo_mine = pieces[:, q_rows:].reshape(D, half_rows)
    wq_other, wo_other = lax.ppermute((wq_mine, wo_mine), "tc", [(0, 1), (1, 0)])
    gate_up_full = lax.all_gather(w_gate_up, TOK, axis=1, tiled=True)
    down_full = lax.all_gather(w_down, TOK, axis=1, tiled=True)

    normed = rms_norm(hidden_states, first_gain)
    length = cached_len[local_req]
    positions = length + block * tok_rows + jnp.arange(tok_rows, dtype=jnp.int32)
    keyval = jnp.dot(normed, w_keyval, preferred_element_type=jnp.float32)
    new_kv = jnp.concatenate(
        [rotate(keyval[:, :kv_cols], positions), keyval[:, kv_cols:]], axis=1
    ).astype(jnp.bfloat16)
    request_kv = gather_rows(new_kv, "rb", lax.axis_size("rb")).reshape(NEW, 2 * kv_cols)
    other_core = 1 - core
    q_wide = jnp.dot(
        lax.dynamic_slice_in_dim(normed, core * half_rows, half_rows, 1),
        wq_mine,
        preferred_element_type=jnp.float32,
    ) + jnp.dot(
        lax.dynamic_slice_in_dim(normed, other_core * half_rows, half_rows, 1),
        wq_other,
        preferred_element_type=jnp.float32,
    )
    queries = rotate(q_wide, positions).astype(jnp.bfloat16)

    local_pages = page_table[local_req] - lax.axis_index(TOK) * kv_cache.shape[0]
    cached = jnp.take(kv_cache, local_pages, axis=0).reshape(MAX_CACHED, 2 * kv_cols)
    keys_total = jnp.concatenate([cached[:, :kv_cols], request_kv[:, :kv_cols]], axis=0).reshape(
        MAX_CACHED + NEW, KV_HEADS, HEAD_DIM
    )
    values_total = jnp.concatenate(
        [cached[:, kv_cols:], request_kv[:, kv_cols:]], axis=0
    ).reshape(MAX_CACHED + NEW, KV_HEADS, HEAD_DIM)
    grouped_q = queries.reshape(tok_rows, KV_HEADS, group_size, HEAD_DIM)
    scores = (
        jnp.einsum("qgpd,kgd->gpqk", grouped_q, keys_total, preferred_element_type=jnp.float32)
        * ATTN_SCALE
    )
    key_index = jnp.arange(MAX_CACHED + NEW, dtype=jnp.int32)
    query_pos = block * tok_rows + jnp.arange(tok_rows, dtype=jnp.int32)
    allowed = jnp.where(
        key_index[None, :] < MAX_CACHED,
        key_index[None, :] < length,
        key_index[None, :] - MAX_CACHED <= query_pos[:, None],
    )
    scores = jnp.where(allowed, scores, -1e30)
    top_score = jnp.max(scores, axis=-1, keepdims=True)
    weights = jnp.exp(scores - top_score)
    probs = (weights / jnp.sum(weights, axis=-1, keepdims=True)).astype(jnp.bfloat16)
    attended = (
        jnp.einsum("gpqk,kgd->qgpd", probs, values_total, preferred_element_type=jnp.float32)
        .astype(jnp.bfloat16)
        .reshape(tok_rows, HEADS * HEAD_DIM)
    )
    out_mine = jnp.dot(attended, wo_mine, preferred_element_type=jnp.float32)
    out_other = jnp.dot(attended, wo_other, preferred_element_type=jnp.float32)
    first = core == 0
    projected_out = jnp.concatenate(
        [jnp.where(first, out_mine, out_other), jnp.where(first, out_other, out_mine)], axis=1
    )
    middle = (hidden_states.astype(jnp.float32) + projected_out).astype(jnp.bfloat16)
    normed_two = rms_norm(middle, second_gain)

    experts_local = EXPERTS // tp_size
    capacity = 2 * tok_rows * TOP // EXPERTS
    expert_range = jnp.arange(EXPERTS, dtype=jnp.int32)
    onehot = (expert_ids[:, :, None] == expert_range[None, None, :]).astype(jnp.int32)
    per_token = jnp.sum(onehot, axis=1)
    earlier = jnp.cumsum(per_token, axis=0) - per_token
    slot_ids = jnp.sum(onehot * earlier[:, None, :], axis=2)
    target = expert_ids * capacity + slot_ids
    outgoing_rows = jnp.broadcast_to(normed_two[:, None, :], (tok_rows, TOP, D))
    send_buffer = jnp.zeros((EXPERTS * capacity, D), jnp.bfloat16).at[target].set(outgoing_rows)
    send_buffer = send_buffer.reshape(tp_size, experts_local, capacity, D)
    returned = []
    for local in range(experts_local):
        received = lax.all_to_all(
            send_buffer[:, local], TP, split_axis=0, concat_axis=0, tiled=True
        ).reshape(tp_size * capacity, D)
        both = jnp.dot(received, gate_up_full[local], preferred_element_type=jnp.float32)
        activated = (jax.nn.silu(both[:, :FF_EXPERT]) * both[:, FF_EXPERT:]).astype(jnp.bfloat16)
        produced = jnp.dot(
            activated, down_full[local], preferred_element_type=jnp.float32
        ).astype(jnp.bfloat16)
        returned.append(
            lax.all_to_all(
                produced.reshape(tp_size, capacity, D), TP, split_axis=0, concat_axis=0, tiled=True
            )
        )
    returned = jnp.stack(returned, axis=1)
    returned = returned.reshape(EXPERTS * capacity, D)
    picked = returned[target]
    mixture = jnp.einsum("tk,tkd->td", gate_weights, picked.astype(jnp.float32))
    return (middle.astype(jnp.float32) + mixture).astype(jnp.bfloat16)


def solution(mesh):
    tok_size, tp_size = mesh.devices.shape
    group = tp_size // REQ_DEV
    split = Mesh(mesh.devices.reshape(tok_size // 2, 2, REQ_DEV, group), TOK + TP)
    in_specs = (
        P(TOK + TP, None),
        P(),
        P(),
        P(None, TP),
        P(),
        P(TP, None),
        P(TOK, None, None),
        P(TOK, None),
        P(TOK),
        P(TOK + TP, None),
        P(TOK + TP, None),
        P(TP, TOK, None),
        P(TP, TOK, None),
    )
    out_specs = P(TOK + TP, None)
    return jax.shard_map(shards, mesh=split, in_specs=in_specs, out_specs=out_specs, check_vma=False)
```

```python
import jax
import jax.numpy as jnp
from jax import lax
from jax.sharding import Mesh
from jax.sharding import PartitionSpec as P

D = 1024
HEADS = 16
KV_HEADS = 8
HEAD_DIM = 64
EXPERTS = 32
FF_EXPERT = 512
TOP = 8
NEW = 1024
MAX_CACHED = 2048
REQ_DEV = 2


ATTN_SCALE = 0.015625
EPSILON = 1e-06
THETA = 10000.0

TOK = ("tz", "tc")
TP = ("ra", "rb")


def rms_norm(values, gain):
    wide = values.astype(jnp.float32)
    factor = lax.rsqrt(jnp.mean(wide * wide, axis=-1, keepdims=True) + EPSILON)
    return (wide * factor * gain).astype(jnp.bfloat16)


def rotate(values, positions):
    row_count = values.shape[0]
    shaped = values.reshape(row_count, -1, HEAD_DIM)
    half_dim = HEAD_DIM // 2
    exponent = jnp.arange(half_dim).astype(jnp.float32) * (2.0 / HEAD_DIM)
    frequency = jnp.power(THETA, -exponent)
    angles = positions.astype(jnp.float32)[:, None] * frequency[None, :]
    cosine = jnp.cos(angles)[:, None, :]
    sine_part = jnp.sin(angles)[:, None, :]
    leading = shaped[..., :half_dim]
    trailing = shaped[..., half_dim:]
    turned = jnp.concatenate(
        [leading * cosine - trailing * sine_part, trailing * cosine + leading * sine_part], axis=-1
    )
    return turned.reshape(row_count, -1)


def gather_rows(piece, axis_name, count):
    send = jnp.broadcast_to(piece[None], (count,) + piece.shape)
    return lax.all_to_all(send, axis_name, split_axis=0, concat_axis=0, tiled=True)


def shards(
    hidden_states,
    first_gain,
    second_gain,
    w_query,
    w_keyval,
    w_out,
    kv_cache,
    page_table,
    cached_len,
    expert_ids,
    gate_weights,
    w_gate_up,
    w_down,
):
    tok_rows = hidden_states.shape[0]
    tp_size = lax.axis_size(TP)
    core = lax.axis_index("tc")
    local_req = lax.axis_index("ra")
    block = lax.axis_index("rb")
    kv_cols = KV_HEADS * HEAD_DIM
    group_size = HEADS // KV_HEADS

    half_rows = D // 2
    wq_half = lax.dynamic_slice_in_dim(w_query, core * half_rows, half_rows, 0)
    wo_half = lax.dynamic_slice_in_dim(w_out, core * half_rows, half_rows, 1)
    lanes = 128
    pieces = gather_rows(
        jnp.concatenate([wq_half.reshape(-1, lanes), wo_half.reshape(-1, lanes)], axis=0),
        TP,
        tp_size,
    )
    q_rows = wq_half.size // lanes
    wq_mine = jnp.transpose(
        pieces[:, :q_rows].reshape(tp_size, half_rows, HEAD_DIM), (1, 0, 2)
    ).reshape(half_rows, D)
    wo_mine = pieces[:, q_rows:].reshape(D, half_rows)
    wq_other, wo_other = lax.ppermute((wq_mine, wo_mine), "tc", [(0, 1), (1, 0)])
    gate_up_full = lax.all_gather(w_gate_up, TOK, axis=1, tiled=True)
    down_full = lax.all_gather(w_down, TOK, axis=1, tiled=True)

    normed = rms_norm(hidden_states, first_gain)
    length = cached_len[local_req]
    positions = length + block * tok_rows + jnp.arange(tok_rows, dtype=jnp.int32)
    keyval = jnp.dot(normed, w_keyval, preferred_element_type=jnp.float32)
    new_kv = jnp.concatenate(
        [rotate(keyval[:, :kv_cols], positions), keyval[:, kv_cols:]], axis=1
    ).astype(jnp.bfloat16)
    request_kv = gather_rows(new_kv, "rb", lax.axis_size("rb")).reshape(NEW, 2 * kv_cols)
    other_core = 1 - core
    q_wide = jnp.dot(
        lax.dynamic_slice_in_dim(normed, core * half_rows, half_rows, 1),
        wq_mine,
        preferred_element_type=jnp.float32,
    ) + jnp.dot(
        lax.dynamic_slice_in_dim(normed, other_core * half_rows, half_rows, 1),
        wq_other,
        preferred_element_type=jnp.float32,
    )
    queries = rotate(q_wide, positions).astype(jnp.bfloat16)

    local_pages = page_table[local_req] - lax.axis_index(TOK) * kv_cache.shape[0]
    cached = jnp.take(kv_cache, local_pages, axis=0).reshape(MAX_CACHED, 2 * kv_cols)
    keys_total = jnp.concatenate([cached[:, :kv_cols], request_kv[:, :kv_cols]], axis=0).reshape(
        MAX_CACHED + NEW, KV_HEADS, HEAD_DIM
    )
    values_total = jnp.concatenate(
        [cached[:, kv_cols:], request_kv[:, kv_cols:]], axis=0
    ).reshape(MAX_CACHED + NEW, KV_HEADS, HEAD_DIM)
    grouped_q = queries.reshape(tok_rows, KV_HEADS, group_size, HEAD_DIM)
    scores = (
        jnp.einsum("qgpd,kgd->gpqk", grouped_q, keys_total, preferred_element_type=jnp.float32)
        * ATTN_SCALE
    )
    key_index = jnp.arange(MAX_CACHED + NEW, dtype=jnp.int32)
    query_pos = block * tok_rows + jnp.arange(tok_rows, dtype=jnp.int32)
    allowed = jnp.where(
        key_index[None, :] < MAX_CACHED,
        key_index[None, :] < length,
        key_index[None, :] - MAX_CACHED <= query_pos[:, None],
    )
    scores = jnp.where(allowed, scores, -1e30)
    top_score = jnp.max(scores, axis=-1, keepdims=True)
    weights = jnp.exp(scores - top_score)
    probs = (weights / jnp.sum(weights, axis=-1, keepdims=True)).astype(jnp.bfloat16)
    attended = (
        jnp.einsum("gpqk,kgd->qgpd", probs, values_total, preferred_element_type=jnp.float32)
        .astype(jnp.bfloat16)
        .reshape(tok_rows, HEADS * HEAD_DIM)
    )
    out_mine = jnp.dot(attended, wo_mine, preferred_element_type=jnp.float32)
    out_other = jnp.dot(attended, wo_other, preferred_element_type=jnp.float32)
    first = core == 0
    projected_out = jnp.concatenate(
        [jnp.where(first, out_mine, out_other), jnp.where(first, out_other, out_mine)], axis=1
    )
    middle = (hidden_states.astype(jnp.float32) + projected_out).astype(jnp.bfloat16)
    normed_two = rms_norm(middle, second_gain)

    experts_local = EXPERTS // tp_size
    capacity = 2 * tok_rows * TOP // EXPERTS
    expert_range = jnp.arange(EXPERTS, dtype=jnp.int32)
    onehot = (expert_ids[:, :, None] == expert_range[None, None, :]).astype(jnp.int32)
    per_token = jnp.sum(onehot, axis=1)
    earlier = jnp.cumsum(per_token, axis=0) - per_token
    slot_ids = jnp.sum(onehot * earlier[:, None, :], axis=2)
    target = expert_ids * capacity + slot_ids
    slot_range = jnp.arange(EXPERTS * capacity, dtype=jnp.int32)
    hits = target[None, :, :] == slot_range[:, None, None]
    choose = jnp.any(hits, axis=2).astype(jnp.bfloat16)
    send_buffer = (
        jnp.dot(choose, normed_two, preferred_element_type=jnp.float32)
        .astype(jnp.bfloat16)
        .reshape(tp_size, experts_local, capacity, D)
    )
    returned = []
    for local in range(experts_local):
        received = lax.all_to_all(
            send_buffer[:, local], TP, split_axis=0, concat_axis=0, tiled=True
        ).reshape(tp_size * capacity, D)
        both = jnp.dot(received, gate_up_full[local], preferred_element_type=jnp.float32)
        activated = (jax.nn.silu(both[:, :FF_EXPERT]) * both[:, FF_EXPERT:]).astype(jnp.bfloat16)
        produced = jnp.dot(
            activated, down_full[local], preferred_element_type=jnp.float32
        ).astype(jnp.bfloat16)
        returned.append(
            lax.all_to_all(
                produced.reshape(tp_size, capacity, D), TP, split_axis=0, concat_axis=0, tiled=True
            )
        )
    returned = jnp.stack(returned, axis=1)
    returned = returned.reshape(EXPERTS * capacity, D)
    mixing = jnp.sum(
        jnp.where(hits, gate_weights[None, :, :], 0.0), axis=2
    ).T
    mixture = jnp.dot(
        mixing,
        returned.astype(jnp.float32),
        precision=lax.Precision.HIGHEST,
        preferred_element_type=jnp.float32,
    )
    return (middle.astype(jnp.float32) + mixture).astype(jnp.bfloat16)


def solution(mesh):
    tok_size, tp_size = mesh.devices.shape
    group = tp_size // REQ_DEV
    split = Mesh(mesh.devices.reshape(tok_size // 2, 2, REQ_DEV, group), TOK + TP)
    in_specs = (
        P(TOK + TP, None),
        P(),
        P(),
        P(None, TP),
        P(),
        P(TP, None),
        P(TOK, None, None),
        P(TOK, None),
        P(TOK),
        P(TOK + TP, None),
        P(TOK + TP, None),
        P(TP, TOK, None),
        P(TP, TOK, None),
    )
    out_specs = P(TOK + TP, None)
    return jax.shard_map(shards, mesh=split, in_specs=in_specs, out_specs=out_specs, check_vma=False)
```

```python
import jax
import jax.numpy as jnp
from jax import lax
from jax.experimental import pallas as pl
from jax.experimental.pallas import tpu as pltpu
from jax.sharding import Mesh
from jax.sharding import PartitionSpec as P

D = 1024
HEADS = 16
KV_HEADS = 8
HEAD_DIM = 64
EXPERTS = 32
FF_EXPERT = 512
TOP = 8
NEW = 1024
MAX_CACHED = 2048
REQ_DEV = 2


ATTN_SCALE = 0.015625
EPSILON = 1e-06
THETA = 10000.0

TOK = ("tz", "tc")
TP = ("ra", "rb")


def rms_norm(values, gain):
    wide = values.astype(jnp.float32)
    factor = lax.rsqrt(jnp.mean(wide * wide, axis=-1, keepdims=True) + EPSILON)
    return (wide * factor * gain).astype(jnp.bfloat16)


def rotate(values, positions):
    row_count = values.shape[0]
    shaped = values.reshape(row_count, -1, HEAD_DIM)
    half_dim = HEAD_DIM // 2
    exponent = jnp.arange(half_dim).astype(jnp.float32) * (2.0 / HEAD_DIM)
    frequency = jnp.power(THETA, -exponent)
    angles = positions.astype(jnp.float32)[:, None] * frequency[None, :]
    cosine = jnp.cos(angles)[:, None, :]
    sine_part = jnp.sin(angles)[:, None, :]
    leading = shaped[..., :half_dim]
    trailing = shaped[..., half_dim:]
    turned = jnp.concatenate(
        [leading * cosine - trailing * sine_part, trailing * cosine + leading * sine_part], axis=-1
    )
    return turned.reshape(row_count, -1)


def attention_kernel(meta, q_ref, kc_ref, vc_ref, kn_ref, vn_ref, o_ref):
    length = meta[0]
    first_query = meta[1]
    query = q_ref[0]
    rows = query.shape[0]
    contract = (((1,), (1,)), ((), ()))
    s_old = lax.dot_general(query, kc_ref[0], contract, preferred_element_type=jnp.float32) * ATTN_SCALE
    s_new = lax.dot_general(query, kn_ref[0], contract, preferred_element_type=jnp.float32) * ATTN_SCALE
    old_index = lax.broadcasted_iota(jnp.int32, s_old.shape, 1)
    s_old = jnp.where(old_index < length, s_old, -1e30)
    new_index = lax.broadcasted_iota(jnp.int32, s_new.shape, 1)
    query_index = lax.broadcasted_iota(jnp.int32, s_new.shape, 0) % (rows // 2) + first_query
    s_new = jnp.where(new_index <= query_index, s_new, -1e30)
    top = jnp.maximum(jnp.max(s_old, axis=1, keepdims=True), jnp.max(s_new, axis=1, keepdims=True))
    e_old = jnp.exp(s_old - top)
    e_new = jnp.exp(s_new - top)
    total = jnp.sum(e_old, axis=1, keepdims=True) + jnp.sum(e_new, axis=1, keepdims=True)
    p_old = (e_old / total).astype(jnp.bfloat16)
    p_new = (e_new / total).astype(jnp.bfloat16)
    mixed = jnp.dot(p_old, vc_ref[0], preferred_element_type=jnp.float32) + jnp.dot(
        p_new, vn_ref[0], preferred_element_type=jnp.float32
    )
    o_ref[0] = mixed.astype(o_ref.dtype)


def attend(meta, q, kc, vc, kn, vn):
    groups, rows, _ = q.shape
    old = kc.shape[1]
    new = kn.shape[1]
    spec = lambda n: pl.BlockSpec((1, n, HEAD_DIM), lambda c, m: (c, 0, 0))
    return pl.pallas_call(
        attention_kernel,
        grid_spec=pltpu.PrefetchScalarGridSpec(
            num_scalar_prefetch=1,
            grid=(groups,),
            in_specs=[spec(rows), spec(old), spec(old), spec(new), spec(new)],
            out_specs=spec(rows),
        ),
        out_shape=jax.ShapeDtypeStruct(q.shape, jnp.bfloat16),
    )(meta, q, kc, vc, kn, vn)


def gather_rows(piece, axis_name, count):
    send = jnp.broadcast_to(piece[None], (count,) + piece.shape)
    return lax.all_to_all(send, axis_name, split_axis=0, concat_axis=0, tiled=True)


def shards(
    hidden_states,
    first_gain,
    second_gain,
    w_query,
    w_keyval,
    w_out,
    kv_cache,
    page_table,
    cached_len,
    expert_ids,
    gate_weights,
    w_gate_up,
    w_down,
):
    tok_rows = hidden_states.shape[0]
    tp_size = lax.axis_size(TP)
    core = lax.axis_index("tc")
    local_req = lax.axis_index("ra")
    block = lax.axis_index("rb")
    kv_cols = KV_HEADS * HEAD_DIM
    group_size = HEADS // KV_HEADS

    half_rows = D // 2
    wq_half = lax.dynamic_slice_in_dim(w_query, core * half_rows, half_rows, 0)
    wo_half = lax.dynamic_slice_in_dim(w_out, core * half_rows, half_rows, 1)
    lanes = 128
    pieces = gather_rows(
        jnp.concatenate([wq_half.reshape(-1, lanes), wo_half.reshape(-1, lanes)], axis=0),
        TP,
        tp_size,
    )
    q_rows = wq_half.size // lanes
    wq_mine = jnp.transpose(
        pieces[:, :q_rows].reshape(tp_size, half_rows, HEAD_DIM), (1, 0, 2)
    ).reshape(half_rows, D)
    wo_mine = pieces[:, q_rows:].reshape(D, half_rows)
    wq_other, wo_other = lax.ppermute((wq_mine, wo_mine), "tc", [(0, 1), (1, 0)])
    gate_up_full = lax.all_gather(w_gate_up, TOK, axis=1, tiled=True)
    down_full = lax.all_gather(w_down, TOK, axis=1, tiled=True)

    normed = rms_norm(hidden_states, first_gain)
    length = cached_len[local_req]
    positions = length + block * tok_rows + jnp.arange(tok_rows, dtype=jnp.int32)
    keyval = jnp.dot(normed, w_keyval, preferred_element_type=jnp.float32)
    new_kv = jnp.concatenate(
        [rotate(keyval[:, :kv_cols], positions), keyval[:, kv_cols:]], axis=1
    ).astype(jnp.bfloat16)
    request_kv = gather_rows(new_kv, "rb", lax.axis_size("rb")).reshape(NEW, 2 * kv_cols)
    other_core = 1 - core
    q_wide = jnp.dot(
        lax.dynamic_slice_in_dim(normed, core * half_rows, half_rows, 1),
        wq_mine,
        preferred_element_type=jnp.float32,
    ) + jnp.dot(
        lax.dynamic_slice_in_dim(normed, other_core * half_rows, half_rows, 1),
        wq_other,
        preferred_element_type=jnp.float32,
    )
    queries = rotate(q_wide, positions).astype(jnp.bfloat16)

    local_pages = page_table[local_req] - lax.axis_index(TOK) * kv_cache.shape[0]
    cached = jnp.take(kv_cache, local_pages, axis=0).reshape(MAX_CACHED, 2 * kv_cols)
    def heads_major(rows):
        return rows.reshape(rows.shape[0], 2, KV_HEADS, HEAD_DIM).transpose(1, 2, 0, 3)

    cached_heads = heads_major(cached)
    new_heads = heads_major(request_kv)
    grouped_q = (
        queries.reshape(tok_rows, KV_HEADS, group_size, HEAD_DIM)
        .transpose(1, 2, 0, 3)
        .reshape(KV_HEADS, group_size * tok_rows, HEAD_DIM)
    )
    meta = jnp.stack([length, block * tok_rows]).astype(jnp.int32)
    mixed = attend(meta, grouped_q, cached_heads[0], cached_heads[1], new_heads[0], new_heads[1])
    attended = (
        mixed.reshape(KV_HEADS, group_size, tok_rows, HEAD_DIM)
        .transpose(2, 0, 1, 3)
        .reshape(tok_rows, HEADS * HEAD_DIM)
    )
    out_mine = jnp.dot(attended, wo_mine, preferred_element_type=jnp.float32)
    out_other = jnp.dot(attended, wo_other, preferred_element_type=jnp.float32)
    first = core == 0
    projected_out = jnp.concatenate(
        [jnp.where(first, out_mine, out_other), jnp.where(first, out_other, out_mine)], axis=1
    )
    middle = (hidden_states.astype(jnp.float32) + projected_out).astype(jnp.bfloat16)
    normed_two = rms_norm(middle, second_gain)

    experts_local = EXPERTS // tp_size
    capacity = 2 * tok_rows * TOP // EXPERTS
    expert_range = jnp.arange(EXPERTS, dtype=jnp.int32)
    onehot = (expert_ids[:, :, None] == expert_range[None, None, :]).astype(jnp.int32)
    per_token = jnp.sum(onehot, axis=1)
    earlier = jnp.cumsum(per_token, axis=0) - per_token
    slot_ids = jnp.sum(onehot * earlier[:, None, :], axis=2)
    target = expert_ids * capacity + slot_ids
    slot_range = jnp.arange(EXPERTS * capacity, dtype=jnp.int32)
    hits = target[None, :, :] == slot_range[:, None, None]
    choose = jnp.any(hits, axis=2).astype(jnp.bfloat16)
    send_buffer = (
        jnp.dot(choose, normed_two, preferred_element_type=jnp.float32)
        .astype(jnp.bfloat16)
        .reshape(tp_size, experts_local, capacity, D)
    )
    returned = []
    for local in range(experts_local):
        received = lax.all_to_all(
            send_buffer[:, local], TP, split_axis=0, concat_axis=0, tiled=True
        ).reshape(tp_size * capacity, D)
        both = jnp.dot(received, gate_up_full[local], preferred_element_type=jnp.float32)
        activated = (jax.nn.silu(both[:, :FF_EXPERT]) * both[:, FF_EXPERT:]).astype(jnp.bfloat16)
        produced = jnp.dot(
            activated, down_full[local], preferred_element_type=jnp.float32
        ).astype(jnp.bfloat16)
        returned.append(
            lax.all_to_all(
                produced.reshape(tp_size, capacity, D), TP, split_axis=0, concat_axis=0, tiled=True
            )
        )
    returned = jnp.stack(returned, axis=1)
    returned = returned.reshape(EXPERTS * capacity, D)
    mixing = jnp.sum(
        jnp.where(hits, gate_weights[None, :, :], 0.0), axis=2
    ).T
    mixture = jnp.dot(
        mixing,
        returned.astype(jnp.float32),
        precision=lax.Precision.HIGHEST,
        preferred_element_type=jnp.float32,
    )
    return (middle.astype(jnp.float32) + mixture).astype(jnp.bfloat16)


def solution(mesh):
    tok_size, tp_size = mesh.devices.shape
    group = tp_size // REQ_DEV
    split = Mesh(mesh.devices.reshape(tok_size // 2, 2, REQ_DEV, group), TOK + TP)
    in_specs = (
        P(TOK + TP, None),
        P(),
        P(),
        P(None, TP),
        P(),
        P(TP, None),
        P(TOK, None, None),
        P(TOK, None),
        P(TOK),
        P(TOK + TP, None),
        P(TOK + TP, None),
        P(TP, TOK, None),
        P(TP, TOK, None),
    )
    out_specs = P(TOK + TP, None)
    return jax.shard_map(shards, mesh=split, in_specs=in_specs, out_specs=out_specs, check_vma=False)
```

```python
import jax
import jax.numpy as jnp
from jax import lax
from jax.experimental import pallas as pl
from jax.experimental.pallas import tpu as pltpu
from jax.sharding import Mesh
from jax.sharding import PartitionSpec as P

D = 1024
HEADS = 16
KV_HEADS = 8
HEAD_DIM = 64
EXPERTS = 32
FF_EXPERT = 512
TOP = 8
NEW = 1024
MAX_CACHED = 2048
REQ_DEV = 2


ATTN_SCALE = 0.015625
EPSILON = 1e-06
THETA = 10000.0


TOK = ("tz", "tc")
TP = ("ra", "rb")


def rms_norm(values, gain):
    wide = values.astype(jnp.float32)
    factor = lax.rsqrt(jnp.mean(wide * wide, axis=-1, keepdims=True) + EPSILON)
    return (wide * factor * gain).astype(jnp.bfloat16)


def rotate(values, positions):
    row_count = values.shape[0]
    shaped = values.reshape(row_count, -1, HEAD_DIM)
    half_dim = HEAD_DIM // 2
    exponent = jnp.arange(half_dim).astype(jnp.float32) * (2.0 / HEAD_DIM)
    frequency = jnp.power(THETA, -exponent)
    angles = positions.astype(jnp.float32)[:, None] * frequency[None, :]
    cosine = jnp.cos(angles)[:, None, :]
    sine_part = jnp.sin(angles)[:, None, :]
    leading = shaped[..., :half_dim]
    trailing = shaped[..., half_dim:]
    turned = jnp.concatenate(
        [leading * cosine - trailing * sine_part, trailing * cosine + leading * sine_part], axis=-1
    )
    return turned.reshape(row_count, -1)


def attention_kernel(meta, q_ref, kc_ref, vc_ref, kn_ref, vn_ref, o_ref):
    length = meta[0]
    first_query = meta[1]
    query = q_ref[0]
    rows = query.shape[0]
    contract = (((1,), (1,)), ((), ()))
    s_old = lax.dot_general(query, kc_ref[0], contract, preferred_element_type=jnp.float32) * ATTN_SCALE
    s_new = lax.dot_general(query, kn_ref[0], contract, preferred_element_type=jnp.float32) * ATTN_SCALE
    old_index = lax.broadcasted_iota(jnp.int32, s_old.shape, 1)
    s_old = jnp.where(old_index < length, s_old, -1e30)
    new_index = lax.broadcasted_iota(jnp.int32, s_new.shape, 1)
    query_index = lax.broadcasted_iota(jnp.int32, s_new.shape, 0) % (rows // 2) + first_query
    s_new = jnp.where(new_index <= query_index, s_new, -1e30)
    top = jnp.maximum(jnp.max(s_old, axis=1, keepdims=True), jnp.max(s_new, axis=1, keepdims=True))
    e_old = jnp.exp(s_old - top)
    e_new = jnp.exp(s_new - top)
    total = jnp.sum(e_old, axis=1, keepdims=True) + jnp.sum(e_new, axis=1, keepdims=True)
    p_old = (e_old / total).astype(jnp.bfloat16)
    p_new = (e_new / total).astype(jnp.bfloat16)
    mixed = jnp.dot(p_old, vc_ref[0], preferred_element_type=jnp.float32) + jnp.dot(
        p_new, vn_ref[0], preferred_element_type=jnp.float32
    )
    o_ref[0] = mixed.astype(o_ref.dtype)


def attend(meta, q, kc, vc, kn, vn):
    groups, rows, _ = q.shape
    old = kc.shape[1]
    new = kn.shape[1]
    spec = lambda n: pl.BlockSpec((1, n, HEAD_DIM), lambda c, m: (c, 0, 0))
    return pl.pallas_call(
        attention_kernel,
        grid_spec=pltpu.PrefetchScalarGridSpec(
            num_scalar_prefetch=1,
            grid=(groups,),
            in_specs=[spec(rows), spec(old), spec(old), spec(new), spec(new)],
            out_specs=spec(rows),
        ),
        out_shape=jax.ShapeDtypeStruct(q.shape, jnp.bfloat16),
    )(meta, q, kc, vc, kn, vn)


def gather_rows(piece, axis_name, count):
    send = jnp.broadcast_to(piece[None], (count,) + piece.shape)
    return lax.all_to_all(send, axis_name, split_axis=0, concat_axis=0, tiled=True)


def shards(
    hidden_states,
    first_gain,
    second_gain,
    w_query,
    w_keyval,
    w_out,
    kv_cache,
    page_table,
    cached_len,
    expert_ids,
    gate_weights,
    w_gate_up,
    w_down,
):
    tok_rows = hidden_states.shape[0]
    tp_size = lax.axis_size(TP)
    core = lax.axis_index("tc")
    local_req = lax.axis_index("ra")
    block = lax.axis_index("rb")
    kv_cols = KV_HEADS * HEAD_DIM
    group_size = HEADS // KV_HEADS

    half_rows = D // 2
    wq_half = lax.dynamic_slice_in_dim(w_query, core * half_rows, half_rows, 0)
    wo_half = lax.dynamic_slice_in_dim(w_out, core * half_rows, half_rows, 1)
    lanes = 128
    pieces = gather_rows(
        jnp.concatenate([wq_half.reshape(-1, lanes), wo_half.reshape(-1, lanes)], axis=0),
        TP,
        tp_size,
    )
    q_rows = wq_half.size // lanes
    wq_mine = jnp.transpose(
        pieces[:, :q_rows].reshape(tp_size, half_rows, HEAD_DIM), (1, 0, 2)
    ).reshape(half_rows, D)
    wo_mine = pieces[:, q_rows:].reshape(D, half_rows)
    wq_other, wo_other = lax.ppermute((wq_mine, wo_mine), "tc", [(0, 1), (1, 0)])
    gate_up_full = lax.all_gather(w_gate_up, TOK, axis=1, tiled=True)
    down_full = lax.all_gather(w_down, TOK, axis=1, tiled=True)

    normed = rms_norm(hidden_states, first_gain)
    length = cached_len[local_req]
    positions = length + block * tok_rows + jnp.arange(tok_rows, dtype=jnp.int32)
    keyval = jnp.dot(normed, w_keyval, preferred_element_type=jnp.float32)
    new_kv = jnp.concatenate(
        [rotate(keyval[:, :kv_cols], positions), keyval[:, kv_cols:]], axis=1
    ).astype(jnp.bfloat16)
    request_kv = gather_rows(new_kv, "rb", lax.axis_size("rb")).reshape(NEW, 2 * kv_cols)
    other_core = 1 - core
    q_wide = jnp.dot(
        lax.dynamic_slice_in_dim(normed, core * half_rows, half_rows, 1),
        wq_mine,
        preferred_element_type=jnp.float32,
    ) + jnp.dot(
        lax.dynamic_slice_in_dim(normed, other_core * half_rows, half_rows, 1),
        wq_other,
        preferred_element_type=jnp.float32,
    )
    queries = rotate(q_wide, positions).astype(jnp.bfloat16)

    local_pages = page_table[local_req] - lax.axis_index(TOK) * kv_cache.shape[0]
    cached = jnp.take(kv_cache, local_pages, axis=0).reshape(MAX_CACHED, 2 * kv_cols)
    def heads_major(rows):
        return rows.reshape(rows.shape[0], 2, KV_HEADS, HEAD_DIM).transpose(1, 2, 0, 3)

    cached_heads = heads_major(cached)
    new_heads = heads_major(request_kv)
    grouped_q = (
        queries.reshape(tok_rows, KV_HEADS, group_size, HEAD_DIM)
        .transpose(1, 2, 0, 3)
        .reshape(KV_HEADS, group_size * tok_rows, HEAD_DIM)
    )
    meta = jnp.stack([length, block * tok_rows]).astype(jnp.int32)
    mixed = attend(meta, grouped_q, cached_heads[0], cached_heads[1], new_heads[0], new_heads[1])
    attended = (
        mixed.reshape(KV_HEADS, group_size, tok_rows, HEAD_DIM)
        .transpose(2, 0, 1, 3)
        .reshape(tok_rows, HEADS * HEAD_DIM)
    )
    out_mine = jnp.dot(attended, wo_mine, preferred_element_type=jnp.float32)
    out_other = jnp.dot(attended, wo_other, preferred_element_type=jnp.float32)
    first = core == 0
    projected_out = jnp.concatenate(
        [jnp.where(first, out_mine, out_other), jnp.where(first, out_other, out_mine)], axis=1
    )
    middle = (hidden_states.astype(jnp.float32) + projected_out).astype(jnp.bfloat16)
    normed_two = rms_norm(middle, second_gain)

    experts_local = EXPERTS // tp_size
    capacity = 2 * tok_rows * TOP // EXPERTS
    expert_range = jnp.arange(EXPERTS, dtype=jnp.int32)
    onehot = (expert_ids[:, :, None] == expert_range[None, None, :]).astype(jnp.int32)
    per_token = jnp.sum(onehot, axis=1)
    earlier = jnp.cumsum(per_token, axis=0) - per_token
    slot_ids = jnp.sum(onehot * earlier[:, None, :], axis=2)
    shift = (expert_ids // experts_local - lax.axis_index(TP)) % tp_size
    target = (shift * experts_local + expert_ids % experts_local) * capacity + slot_ids
    slot_range = jnp.arange(EXPERTS * capacity, dtype=jnp.int32)
    hits = target[None, :, :] == slot_range[:, None, None]
    choose = jnp.any(hits, axis=2).astype(jnp.bfloat16)
    send_buffer = (
        jnp.dot(choose, normed_two, preferred_element_type=jnp.float32)
        .astype(jnp.bfloat16)
        .reshape(tp_size, experts_local, capacity, D)
    )
    received = jnp.stack(
        [send_buffer[0]]
        + [
            lax.ppermute(send_buffer[step], TP, [(j, (j + step) % tp_size) for j in range(tp_size)])
            for step in range(1, tp_size)
        ]
    )
    returned = []
    for local in range(experts_local):
        rows = received[:, local].reshape(tp_size * capacity, D)
        both = jnp.dot(rows, gate_up_full[local], preferred_element_type=jnp.float32)
        activated = (jax.nn.silu(both[:, :FF_EXPERT]) * both[:, FF_EXPERT:]).astype(jnp.bfloat16)
        produced = (
            jnp.dot(activated, down_full[local], preferred_element_type=jnp.float32)
            .astype(jnp.bfloat16)
            .reshape(tp_size, capacity, D)
        )
        returned.append(
            jnp.stack(
                [produced[0]]
                + [
                    lax.ppermute(
                        produced[step], TP, [(j, (j - step) % tp_size) for j in range(tp_size)]
                    )
                    for step in range(1, tp_size)
                ]
            )
        )
    returned = jnp.stack(returned, axis=1)
    returned = returned.reshape(EXPERTS * capacity, D)
    mixing = jnp.sum(
        jnp.where(hits, gate_weights[None, :, :], 0.0), axis=2
    ).T
    mixture = jnp.dot(
        mixing,
        returned.astype(jnp.float32),
        precision=lax.Precision.HIGHEST,
        preferred_element_type=jnp.float32,
    )
    return (middle.astype(jnp.float32) + mixture).astype(jnp.bfloat16)


def solution(mesh):
    tok_size, tp_size = mesh.devices.shape
    group = tp_size // REQ_DEV
    split = Mesh(mesh.devices.reshape(tok_size // 2, 2, REQ_DEV, group), TOK + TP)
    in_specs = (
        P(TOK + TP, None),
        P(),
        P(),
        P(None, TP),
        P(),
        P(TP, None),
        P(TOK, None, None),
        P(TOK, None),
        P(TOK),
        P(TOK + TP, None),
        P(TOK + TP, None),
        P(TP, TOK, None),
        P(TP, TOK, None),
    )
    out_specs = P(TOK + TP, None)
    return jax.shard_map(shards, mesh=split, in_specs=in_specs, out_specs=out_specs, check_vma=False)
```

```python
import jax
import jax.numpy as jnp
from jax import lax
from jax.experimental import pallas as pl
from jax.experimental.pallas import tpu as pltpu
from jax.sharding import Mesh
from jax.sharding import PartitionSpec as P

D = 1024
HEADS = 16
KV_HEADS = 8
HEAD_DIM = 64
EXPERTS = 32
FF_EXPERT = 512
TOP = 8
NEW = 1024
MAX_CACHED = 2048
REQ_DEV = 2


ATTN_SCALE = 0.015625
EPSILON = 1e-06
THETA = 10000.0

TOK = ("tz", "tc")
TP = ("ra", "rb")


def rms_norm(values, gain):
    wide = values.astype(jnp.float32)
    factor = lax.rsqrt(jnp.mean(wide * wide, axis=-1, keepdims=True) + EPSILON)
    return (wide * factor * gain).astype(jnp.bfloat16)


def rotate(values, positions):
    row_count = values.shape[0]
    shaped = values.reshape(row_count, -1, HEAD_DIM)
    half_dim = HEAD_DIM // 2
    exponent = jnp.arange(half_dim).astype(jnp.float32) * (2.0 / HEAD_DIM)
    frequency = jnp.power(THETA, -exponent)
    angles = positions.astype(jnp.float32)[:, None] * frequency[None, :]
    cosine = jnp.cos(angles)[:, None, :]
    sine_part = jnp.sin(angles)[:, None, :]
    leading = shaped[..., :half_dim]
    trailing = shaped[..., half_dim:]
    turned = jnp.concatenate(
        [leading * cosine - trailing * sine_part, trailing * cosine + leading * sine_part], axis=-1
    )
    return turned.reshape(row_count, -1)


def attention_kernel(meta, q_ref, kc_ref, vc_ref, kn_ref, vn_ref, o_ref):
    length = meta[0]
    first_query = meta[1]
    query = q_ref[0]
    rows = query.shape[0]
    contract = (((1,), (1,)), ((), ()))
    s_old = lax.dot_general(query, kc_ref[...], contract, preferred_element_type=jnp.float32) * ATTN_SCALE
    s_new = lax.dot_general(query, kn_ref[...], contract, preferred_element_type=jnp.float32) * ATTN_SCALE
    old_index = lax.broadcasted_iota(jnp.int32, s_old.shape, 1)
    s_old = jnp.where(old_index < length, s_old, -1e30)
    new_index = lax.broadcasted_iota(jnp.int32, s_new.shape, 1)
    query_index = lax.broadcasted_iota(jnp.int32, s_new.shape, 0) % (rows // 2) + first_query
    s_new = jnp.where(new_index <= query_index, s_new, -1e30)
    top = jnp.maximum(jnp.max(s_old, axis=1, keepdims=True), jnp.max(s_new, axis=1, keepdims=True))
    e_old = jnp.exp(s_old - top)
    e_new = jnp.exp(s_new - top)
    total = jnp.sum(e_old, axis=1, keepdims=True) + jnp.sum(e_new, axis=1, keepdims=True)
    p_old = (e_old / total).astype(jnp.bfloat16)
    p_new = (e_new / total).astype(jnp.bfloat16)
    mixed = jnp.dot(p_old, vc_ref[...], preferred_element_type=jnp.float32) + jnp.dot(
        p_new, vn_ref[...], preferred_element_type=jnp.float32
    )
    o_ref[0] = mixed.astype(o_ref.dtype)


def attend(meta, q, kc, vc, kn, vn):
    groups, rows, _ = q.shape
    old = kc.shape[0]
    new = kn.shape[0]
    lanes = 2 * HEAD_DIM
    values_at = KV_HEADS * HEAD_DIM // lanes
    spec = pl.BlockSpec((1, rows, lanes), lambda c, m: (c, 0, 0))
    keys = lambda n: pl.BlockSpec((n, lanes), lambda c, m: (0, c // 2))
    values = lambda n: pl.BlockSpec((n, lanes), lambda c, m: (0, values_at + c // 2))
    return pl.pallas_call(
        attention_kernel,
        grid_spec=pltpu.PrefetchScalarGridSpec(
            num_scalar_prefetch=1,
            grid=(groups,),
            in_specs=[spec, keys(old), values(old), keys(new), values(new)],
            out_specs=spec,
        ),
        out_shape=jax.ShapeDtypeStruct(q.shape, jnp.bfloat16),
    )(meta, q, kc, vc, kn, vn)


def gather_rows(piece, axis_name, count):
    send = jnp.broadcast_to(piece[None], (count,) + piece.shape)
    return lax.all_to_all(send, axis_name, split_axis=0, concat_axis=0, tiled=True)


def shards(
    hidden_states,
    first_gain,
    second_gain,
    w_query,
    w_keyval,
    w_out,
    kv_cache,
    page_table,
    cached_len,
    expert_ids,
    gate_weights,
    w_gate_up,
    w_down,
):
    tok_rows = hidden_states.shape[0]
    tp_size = lax.axis_size(TP)
    core = lax.axis_index("tc")
    local_req = lax.axis_index("ra")
    block = lax.axis_index("rb")
    kv_cols = KV_HEADS * HEAD_DIM
    group_size = HEADS // KV_HEADS

    half_rows = D // 2
    wq_half = lax.dynamic_slice_in_dim(w_query, core * half_rows, half_rows, 0)
    wo_half = lax.dynamic_slice_in_dim(w_out, core * half_rows, half_rows, 1)
    lanes = 128
    pieces = gather_rows(
        jnp.concatenate([wq_half.reshape(-1, lanes), wo_half.reshape(-1, lanes)], axis=0),
        TP,
        tp_size,
    )
    q_rows = wq_half.size // lanes
    wq_mine = jnp.transpose(
        pieces[:, :q_rows].reshape(tp_size, half_rows, HEAD_DIM), (1, 0, 2)
    ).reshape(half_rows, D)
    wo_mine = pieces[:, q_rows:].reshape(D, half_rows)
    wq_other, wo_other = lax.ppermute((wq_mine, wo_mine), "tc", [(0, 1), (1, 0)])
    gate_up_full = lax.all_gather(w_gate_up, TOK, axis=1, tiled=True)
    down_full = lax.all_gather(w_down, TOK, axis=1, tiled=True)

    normed = rms_norm(hidden_states, first_gain)
    length = cached_len[local_req]
    positions = length + block * tok_rows + jnp.arange(tok_rows, dtype=jnp.int32)
    keyval = jnp.dot(normed, w_keyval, preferred_element_type=jnp.float32)
    new_kv = jnp.concatenate(
        [rotate(keyval[:, :kv_cols], positions), keyval[:, kv_cols:]], axis=1
    ).astype(jnp.bfloat16)
    request_kv = gather_rows(new_kv, "rb", lax.axis_size("rb")).reshape(NEW, 2 * kv_cols)
    other_core = 1 - core
    q_wide = jnp.dot(
        lax.dynamic_slice_in_dim(normed, core * half_rows, half_rows, 1),
        wq_mine,
        preferred_element_type=jnp.float32,
    ) + jnp.dot(
        lax.dynamic_slice_in_dim(normed, other_core * half_rows, half_rows, 1),
        wq_other,
        preferred_element_type=jnp.float32,
    )
    queries = rotate(q_wide, positions).astype(jnp.bfloat16)

    local_pages = page_table[local_req] - lax.axis_index(TOK) * kv_cache.shape[0]
    cached = jnp.take(kv_cache, local_pages, axis=0).reshape(MAX_CACHED, 2 * kv_cols)
    grouped_q = (
        queries.reshape(tok_rows, KV_HEADS, group_size, HEAD_DIM)
        .transpose(1, 2, 0, 3)
        .reshape(KV_HEADS, group_size * tok_rows, HEAD_DIM)
    )
    blank = jnp.zeros_like(grouped_q)
    odd = (jnp.arange(KV_HEADS) % 2 == 1)[:, None, None]
    padded_q = jnp.concatenate(
        [jnp.where(odd, blank, grouped_q), jnp.where(odd, grouped_q, blank)], axis=2
    )
    meta = jnp.stack([length, block * tok_rows]).astype(jnp.int32)
    mixed = attend(meta, padded_q, cached, cached, request_kv, request_kv)
    attended = (
        jnp.where(odd, mixed[:, :, HEAD_DIM:], mixed[:, :, :HEAD_DIM])
        .reshape(KV_HEADS, group_size, tok_rows, HEAD_DIM)
        .transpose(2, 0, 1, 3)
        .reshape(tok_rows, HEADS * HEAD_DIM)
    )
    out_mine = jnp.dot(attended, wo_mine, preferred_element_type=jnp.float32)
    out_other = jnp.dot(attended, wo_other, preferred_element_type=jnp.float32)
    first = core == 0
    projected_out = jnp.concatenate(
        [jnp.where(first, out_mine, out_other), jnp.where(first, out_other, out_mine)], axis=1
    )
    middle = (hidden_states.astype(jnp.float32) + projected_out).astype(jnp.bfloat16)
    normed_two = rms_norm(middle, second_gain)

    experts_local = EXPERTS // tp_size
    capacity = 2 * tok_rows * TOP // EXPERTS
    expert_range = jnp.arange(EXPERTS, dtype=jnp.int32)
    onehot = (expert_ids[:, :, None] == expert_range[None, None, :]).astype(jnp.int32)
    per_token = jnp.sum(onehot, axis=1)
    earlier = jnp.cumsum(per_token, axis=0) - per_token
    slot_ids = jnp.sum(onehot * earlier[:, None, :], axis=2)
    target = expert_ids * capacity + slot_ids
    slot_range = jnp.arange(EXPERTS * capacity, dtype=jnp.int32)
    hits = target[None, :, :] == slot_range[:, None, None]
    choose = jnp.any(hits, axis=2).astype(jnp.bfloat16)
    send_buffer = (
        jnp.dot(choose, normed_two, preferred_element_type=jnp.float32)
        .astype(jnp.bfloat16)
        .reshape(tp_size, experts_local, capacity, D)
    )
    returned = []
    for local in range(experts_local):
        received = lax.all_to_all(
            send_buffer[:, local], TP, split_axis=0, concat_axis=0, tiled=True
        ).reshape(tp_size * capacity, D)
        both = jnp.dot(received, gate_up_full[local], preferred_element_type=jnp.float32)
        activated = (jax.nn.silu(both[:, :FF_EXPERT]) * both[:, FF_EXPERT:]).astype(jnp.bfloat16)
        produced = jnp.dot(
            activated, down_full[local], preferred_element_type=jnp.float32
        ).astype(jnp.bfloat16)
        returned.append(
            lax.all_to_all(
                produced.reshape(tp_size, capacity, D), TP, split_axis=0, concat_axis=0, tiled=True
            )
        )
    returned = jnp.stack(returned, axis=1)
    returned = returned.reshape(EXPERTS * capacity, D)
    mixing = jnp.sum(
        jnp.where(hits, gate_weights[None, :, :], 0.0), axis=2
    ).T
    mixture = jnp.dot(
        mixing,
        returned.astype(jnp.float32),
        precision=lax.Precision.HIGHEST,
        preferred_element_type=jnp.float32,
    )
    return (middle.astype(jnp.float32) + mixture).astype(jnp.bfloat16)


def solution(mesh):
    tok_size, tp_size = mesh.devices.shape
    group = tp_size // REQ_DEV
    split = Mesh(mesh.devices.reshape(tok_size // 2, 2, REQ_DEV, group), TOK + TP)
    in_specs = (
        P(TOK + TP, None),
        P(),
        P(),
        P(None, TP),
        P(),
        P(TP, None),
        P(TOK, None, None),
        P(TOK, None),
        P(TOK),
        P(TOK + TP, None),
        P(TOK + TP, None),
        P(TP, TOK, None),
        P(TP, TOK, None),
    )
    out_specs = P(TOK + TP, None)
    return jax.shard_map(shards, mesh=split, in_specs=in_specs, out_specs=out_specs, check_vma=False)
```

```python
import jax
import jax.numpy as jnp
from jax import lax
from jax.experimental import pallas as pl
from jax.experimental.pallas import tpu as pltpu
from jax.sharding import Mesh
from jax.sharding import PartitionSpec as P

D = 1024
HEADS = 16
KV_HEADS = 8
HEAD_DIM = 64
EXPERTS = 32
FF_EXPERT = 512
TOP = 8
NEW = 1024
MAX_CACHED = 2048
REQ_DEV = 2


ATTN_SCALE = 0.015625
EPSILON = 1e-06
THETA = 10000.0

TOK = ("tz", "tc")
TP = ("ra", "rb")


def rms_norm(values, gain):
    wide = values.astype(jnp.float32)
    factor = lax.rsqrt(jnp.mean(wide * wide, axis=-1, keepdims=True) + EPSILON)
    return (wide * factor * gain).astype(jnp.bfloat16)


def rotate(values, positions):
    row_count = values.shape[0]
    shaped = values.reshape(row_count, -1, HEAD_DIM)
    half_dim = HEAD_DIM // 2
    exponent = jnp.arange(half_dim).astype(jnp.float32) * (2.0 / HEAD_DIM)
    frequency = jnp.power(THETA, -exponent)
    angles = positions.astype(jnp.float32)[:, None] * frequency[None, :]
    cosine = jnp.cos(angles)[:, None, :]
    sine_part = jnp.sin(angles)[:, None, :]
    leading = shaped[..., :half_dim]
    trailing = shaped[..., half_dim:]
    turned = jnp.concatenate(
        [leading * cosine - trailing * sine_part, trailing * cosine + leading * sine_part], axis=-1
    )
    return turned.reshape(row_count, -1)


def attention_kernel(meta, q_ref, kc_ref, vc_ref, kn_ref, vn_ref, o_ref):
    length = meta[0]
    first_query = meta[1]
    query = q_ref[0]
    rows = query.shape[0]
    contract = (((1,), (1,)), ((), ()))
    s_old = lax.dot_general(query, kc_ref[...], contract, preferred_element_type=jnp.float32) * ATTN_SCALE
    s_new = lax.dot_general(query, kn_ref[...], contract, preferred_element_type=jnp.float32) * ATTN_SCALE
    old_index = lax.broadcasted_iota(jnp.int32, s_old.shape, 1)
    s_old = jnp.where(old_index < length, s_old, -1e30)
    new_index = lax.broadcasted_iota(jnp.int32, s_new.shape, 1)
    query_index = lax.broadcasted_iota(jnp.int32, s_new.shape, 0) % (rows // 2) + first_query
    s_new = jnp.where(new_index <= query_index, s_new, -1e30)
    top = jnp.maximum(jnp.max(s_old, axis=1, keepdims=True), jnp.max(s_new, axis=1, keepdims=True))
    e_old = jnp.exp(s_old - top)
    e_new = jnp.exp(s_new - top)
    total = jnp.sum(e_old, axis=1, keepdims=True) + jnp.sum(e_new, axis=1, keepdims=True)
    p_old = (e_old / total).astype(jnp.bfloat16)
    p_new = (e_new / total).astype(jnp.bfloat16)
    mixed = jnp.dot(p_old, vc_ref[...], preferred_element_type=jnp.float32) + jnp.dot(
        p_new, vn_ref[...], preferred_element_type=jnp.float32
    )
    o_ref[0] = mixed.astype(o_ref.dtype)


def attend(meta, q, kc, vc, kn, vn):
    groups, rows, _ = q.shape
    old = kc.shape[0]
    new = kn.shape[0]
    lanes = 2 * HEAD_DIM
    values_at = KV_HEADS * HEAD_DIM // lanes
    spec = pl.BlockSpec((1, rows, lanes), lambda c, m: (c, 0, 0))
    keys = lambda n: pl.BlockSpec((n, lanes), lambda c, m: (0, c // 2))
    values = lambda n: pl.BlockSpec((n, lanes), lambda c, m: (0, values_at + c // 2))
    return pl.pallas_call(
        attention_kernel,
        grid_spec=pltpu.PrefetchScalarGridSpec(
            num_scalar_prefetch=1,
            grid=(groups,),
            in_specs=[spec, keys(old), values(old), keys(new), values(new)],
            out_specs=spec,
        ),
        out_shape=jax.ShapeDtypeStruct(q.shape, jnp.bfloat16),
    )(meta, q, kc, vc, kn, vn)


def gather_rows(piece, axis_name, count):
    send = jnp.broadcast_to(piece[None], (count,) + piece.shape)
    return lax.all_to_all(send, axis_name, split_axis=0, concat_axis=0, tiled=True)


def shards(
    hidden_states,
    first_gain,
    second_gain,
    w_query,
    w_keyval,
    w_out,
    kv_cache,
    page_table,
    cached_len,
    expert_ids,
    gate_weights,
    w_gate_up,
    w_down,
):
    tok_rows = hidden_states.shape[0]
    tp_size = lax.axis_size(TP)
    core = lax.axis_index("tc")
    local_req = lax.axis_index("ra")
    block = lax.axis_index("rb")
    kv_cols = KV_HEADS * HEAD_DIM
    group_size = HEADS // KV_HEADS

    half_rows = D // 2
    wq_half = lax.dynamic_slice_in_dim(w_query, core * half_rows, half_rows, 0)
    wo_half = lax.dynamic_slice_in_dim(w_out, core * half_rows, half_rows, 1)
    gate_up_full = lax.all_gather(w_gate_up, TOK, axis=1, tiled=True)
    down_full = lax.all_gather(w_down, TOK, axis=1, tiled=True)

    normed = rms_norm(hidden_states, first_gain)
    length = cached_len[local_req]
    positions = length + block * tok_rows + jnp.arange(tok_rows, dtype=jnp.int32)
    keyval = jnp.dot(normed, w_keyval, preferred_element_type=jnp.float32)
    new_kv = jnp.concatenate(
        [rotate(keyval[:, :kv_cols], positions), keyval[:, kv_cols:]], axis=1
    ).astype(jnp.bfloat16)
    group = lax.axis_size("rb")
    packed = jnp.concatenate([new_kv, wq_half.reshape(-1, D), wo_half.reshape(-1, D)], axis=0)
    got = gather_rows(packed, "rb", group)
    request_kv = got[:, :tok_rows].reshape(NEW, 2 * kv_cols)
    weight_rows = wq_half.size // D
    wq_near = got[:, tok_rows : tok_rows + weight_rows].reshape(group, half_rows, HEAD_DIM)
    wo_near = got[:, tok_rows + weight_rows :].reshape(group, HEAD_DIM, half_rows)
    wq_far, wo_far = lax.ppermute((wq_near, wo_near), "ra", [(0, 1), (1, 0)])
    lead = local_req == 0
    wq_all = jnp.where(
        lead, jnp.concatenate([wq_near, wq_far]), jnp.concatenate([wq_far, wq_near])
    )
    wo_all = jnp.where(
        lead, jnp.concatenate([wo_near, wo_far]), jnp.concatenate([wo_far, wo_near])
    )
    wq_mine = jnp.transpose(wq_all, (1, 0, 2)).reshape(half_rows, D)
    wo_mine = wo_all.reshape(D, half_rows)
    wq_other, wo_other = lax.ppermute((wq_mine, wo_mine), "tc", [(0, 1), (1, 0)])
    other_core = 1 - core
    q_wide = jnp.dot(
        lax.dynamic_slice_in_dim(normed, core * half_rows, half_rows, 1),
        wq_mine,
        preferred_element_type=jnp.float32,
    ) + jnp.dot(
        lax.dynamic_slice_in_dim(normed, other_core * half_rows, half_rows, 1),
        wq_other,
        preferred_element_type=jnp.float32,
    )
    queries = rotate(q_wide, positions).astype(jnp.bfloat16)

    local_pages = page_table[local_req] - lax.axis_index(TOK) * kv_cache.shape[0]
    cached = jnp.take(kv_cache, local_pages, axis=0).reshape(MAX_CACHED, 2 * kv_cols)
    grouped_q = (
        queries.reshape(tok_rows, KV_HEADS, group_size, HEAD_DIM)
        .transpose(1, 2, 0, 3)
        .reshape(KV_HEADS, group_size * tok_rows, HEAD_DIM)
    )
    blank = jnp.zeros_like(grouped_q)
    odd = (jnp.arange(KV_HEADS) % 2 == 1)[:, None, None]
    padded_q = jnp.concatenate(
        [jnp.where(odd, blank, grouped_q), jnp.where(odd, grouped_q, blank)], axis=2
    )
    meta = jnp.stack([length, block * tok_rows]).astype(jnp.int32)
    mixed = attend(meta, padded_q, cached, cached, request_kv, request_kv)
    attended = (
        jnp.where(odd, mixed[:, :, HEAD_DIM:], mixed[:, :, :HEAD_DIM])
        .reshape(KV_HEADS, group_size, tok_rows, HEAD_DIM)
        .transpose(2, 0, 1, 3)
        .reshape(tok_rows, HEADS * HEAD_DIM)
    )
    out_mine = jnp.dot(attended, wo_mine, preferred_element_type=jnp.float32)
    out_other = jnp.dot(attended, wo_other, preferred_element_type=jnp.float32)
    first = core == 0
    projected_out = jnp.concatenate(
        [jnp.where(first, out_mine, out_other), jnp.where(first, out_other, out_mine)], axis=1
    )
    middle = (hidden_states.astype(jnp.float32) + projected_out).astype(jnp.bfloat16)
    normed_two = rms_norm(middle, second_gain)

    experts_local = EXPERTS // tp_size
    capacity = 2 * tok_rows * TOP // EXPERTS
    expert_range = jnp.arange(EXPERTS, dtype=jnp.int32)
    onehot = (expert_ids[:, :, None] == expert_range[None, None, :]).astype(jnp.int32)
    per_token = jnp.sum(onehot, axis=1)
    earlier = jnp.cumsum(per_token, axis=0) - per_token
    slot_ids = jnp.sum(onehot * earlier[:, None, :], axis=2)
    target = expert_ids * capacity + slot_ids
    slot_range = jnp.arange(EXPERTS * capacity, dtype=jnp.int32)
    hits = target[None, :, :] == slot_range[:, None, None]
    choose = jnp.any(hits, axis=2).astype(jnp.bfloat16)
    send_buffer = (
        jnp.dot(choose, normed_two, preferred_element_type=jnp.float32)
        .astype(jnp.bfloat16)
        .reshape(tp_size, experts_local, capacity, D)
    )
    returned = []
    for local in range(experts_local):
        received = lax.all_to_all(
            send_buffer[:, local], TP, split_axis=0, concat_axis=0, tiled=True
        ).reshape(tp_size * capacity, D)
        both = jnp.dot(received, gate_up_full[local], preferred_element_type=jnp.float32)
        activated = (jax.nn.silu(both[:, :FF_EXPERT]) * both[:, FF_EXPERT:]).astype(jnp.bfloat16)
        produced = jnp.dot(
            activated, down_full[local], preferred_element_type=jnp.float32
        ).astype(jnp.bfloat16)
        returned.append(
            lax.all_to_all(
                produced.reshape(tp_size, capacity, D), TP, split_axis=0, concat_axis=0, tiled=True
            )
        )
    returned = jnp.stack(returned, axis=1)
    returned = returned.reshape(EXPERTS * capacity, D)
    mixing = jnp.sum(
        jnp.where(hits, gate_weights[None, :, :], 0.0), axis=2
    ).T
    mixture = jnp.dot(
        mixing,
        returned.astype(jnp.float32),
        precision=lax.Precision.HIGHEST,
        preferred_element_type=jnp.float32,
    )
    return (middle.astype(jnp.float32) + mixture).astype(jnp.bfloat16)


def solution(mesh):
    tok_size, tp_size = mesh.devices.shape
    group = tp_size // REQ_DEV
    split = Mesh(mesh.devices.reshape(tok_size // 2, 2, REQ_DEV, group), TOK + TP)
    in_specs = (
        P(TOK + TP, None),
        P(),
        P(),
        P(None, TP),
        P(),
        P(TP, None),
        P(TOK, None, None),
        P(TOK, None),
        P(TOK),
        P(TOK + TP, None),
        P(TOK + TP, None),
        P(TP, TOK, None),
        P(TP, TOK, None),
    )
    out_specs = P(TOK + TP, None)
    return jax.shard_map(shards, mesh=split, in_specs=in_specs, out_specs=out_specs, check_vma=False)
```

```python
import jax
import jax.numpy as jnp
from jax import lax
from jax.experimental import pallas as pl
from jax.experimental.pallas import tpu as pltpu
from jax.sharding import Mesh
from jax.sharding import PartitionSpec as P

D = 1024
HEADS = 16
KV_HEADS = 8
HEAD_DIM = 64
EXPERTS = 32
FF_EXPERT = 512
TOP = 8
NEW = 1024
MAX_CACHED = 2048
REQ_DEV = 2


ATTN_SCALE = 0.015625
EPSILON = 1e-06
THETA = 10000.0

TOK = ("tz", "tc")
TP = ("ra", "rb")


def rms_norm(values, gain):
    wide = values.astype(jnp.float32)
    factor = lax.rsqrt(jnp.mean(wide * wide, axis=-1, keepdims=True) + EPSILON)
    return (wide * factor * gain).astype(jnp.bfloat16)


def rotate(values, positions):
    row_count = values.shape[0]
    shaped = values.reshape(row_count, -1, HEAD_DIM)
    half_dim = HEAD_DIM // 2
    exponent = jnp.arange(half_dim).astype(jnp.float32) * (2.0 / HEAD_DIM)
    frequency = jnp.power(THETA, -exponent)
    angles = positions.astype(jnp.float32)[:, None] * frequency[None, :]
    cosine = jnp.cos(angles)[:, None, :]
    sine_part = jnp.sin(angles)[:, None, :]
    leading = shaped[..., :half_dim]
    trailing = shaped[..., half_dim:]
    turned = jnp.concatenate(
        [leading * cosine - trailing * sine_part, trailing * cosine + leading * sine_part], axis=-1
    )
    return turned.reshape(row_count, -1)


def attention_kernel(meta, q_ref, kc_ref, vc_ref, kn_ref, vn_ref, o_ref):
    length = meta[0]
    first_query = meta[1]
    query = q_ref[0]
    rows = query.shape[0]
    contract = (((1,), (1,)), ((), ()))
    s_old = lax.dot_general(query, kc_ref[...], contract, preferred_element_type=jnp.float32) * ATTN_SCALE
    s_new = lax.dot_general(query, kn_ref[...], contract, preferred_element_type=jnp.float32) * ATTN_SCALE
    old_index = lax.broadcasted_iota(jnp.int32, s_old.shape, 1)
    s_old = jnp.where(old_index < length, s_old, -1e30)
    new_index = lax.broadcasted_iota(jnp.int32, s_new.shape, 1)
    query_index = lax.broadcasted_iota(jnp.int32, s_new.shape, 0) % (rows // 2) + first_query
    s_new = jnp.where(new_index <= query_index, s_new, -1e30)
    top = jnp.maximum(jnp.max(s_old, axis=1, keepdims=True), jnp.max(s_new, axis=1, keepdims=True))
    e_old = jnp.exp(s_old - top)
    e_new = jnp.exp(s_new - top)
    total = jnp.sum(e_old, axis=1, keepdims=True) + jnp.sum(e_new, axis=1, keepdims=True)
    p_old = (e_old / total).astype(jnp.bfloat16)
    p_new = (e_new / total).astype(jnp.bfloat16)
    mixed = jnp.dot(p_old, vc_ref[...], preferred_element_type=jnp.float32) + jnp.dot(
        p_new, vn_ref[...], preferred_element_type=jnp.float32
    )
    o_ref[0] = mixed.astype(o_ref.dtype)


def attend(meta, q, kc, vc, kn, vn):
    groups, rows, _ = q.shape
    old = kc.shape[0]
    new = kn.shape[0]
    lanes = 2 * HEAD_DIM
    values_at = KV_HEADS * HEAD_DIM // lanes
    spec = pl.BlockSpec((1, rows, lanes), lambda c, m: (c, 0, 0))
    keys = lambda n: pl.BlockSpec((n, lanes), lambda c, m: (0, c // 2))
    values = lambda n: pl.BlockSpec((n, lanes), lambda c, m: (0, values_at + c // 2))
    return pl.pallas_call(
        attention_kernel,
        grid_spec=pltpu.PrefetchScalarGridSpec(
            num_scalar_prefetch=1,
            grid=(groups,),
            in_specs=[spec, keys(old), values(old), keys(new), values(new)],
            out_specs=spec,
        ),
        out_shape=jax.ShapeDtypeStruct(q.shape, jnp.bfloat16),
    )(meta, q, kc, vc, kn, vn)


def gather_rows(piece, axis_name, count):
    send = jnp.broadcast_to(piece[None], (count,) + piece.shape)
    return lax.all_to_all(send, axis_name, split_axis=0, concat_axis=0, tiled=True)


def shards(
    hidden_states,
    first_gain,
    second_gain,
    w_query,
    w_keyval,
    w_out,
    kv_cache,
    page_table,
    cached_len,
    expert_ids,
    gate_weights,
    w_gate_up,
    w_down,
):
    tok_rows = hidden_states.shape[0]
    tp_size = lax.axis_size(TP)
    core = lax.axis_index("tc")
    local_req = lax.axis_index("ra")
    block = lax.axis_index("rb")
    kv_cols = KV_HEADS * HEAD_DIM
    group_size = HEADS // KV_HEADS

    half_rows = D // 2
    wq_half = lax.dynamic_slice_in_dim(w_query, core * half_rows, half_rows, 0)
    wo_half = lax.dynamic_slice_in_dim(w_out, core * half_rows, half_rows, 1)
    lanes = 128
    quarter = half_rows // 2
    pair_side = lax.axis_index("tz") % 2
    part = (core * 2 + pair_side) * quarter
    wq_part = lax.dynamic_slice_in_dim(w_query, part, quarter, 0)
    wo_part = lax.dynamic_slice_in_dim(w_out, part, quarter, 1)
    pieces = gather_rows(
        jnp.concatenate([wq_part.reshape(-1, lanes), wo_part.reshape(-1, lanes)], axis=0),
        TP,
        tp_size,
    )
    q_rows = wq_part.size // lanes
    wq_near = jnp.transpose(
        pieces[:, :q_rows].reshape(tp_size, quarter, HEAD_DIM), (1, 0, 2)
    ).reshape(quarter, D)
    wo_near = pieces[:, q_rows:].reshape(D, quarter)
    z_pairs = [(j, j ^ 1) for j in range(lax.axis_size("tz"))]
    wq_pair, wo_pair = lax.ppermute((wq_near, wo_near), "tz", z_pairs)
    low = pair_side == 0
    wq_mine = jnp.where(
        low, jnp.concatenate([wq_near, wq_pair]), jnp.concatenate([wq_pair, wq_near])
    )
    wo_mine = jnp.where(
        low,
        jnp.concatenate([wo_near, wo_pair], axis=1),
        jnp.concatenate([wo_pair, wo_near], axis=1),
    )
    wq_other, wo_other = lax.ppermute((wq_mine, wo_mine), "tc", [(0, 1), (1, 0)])
    gate_up_full = lax.all_gather(w_gate_up, TOK, axis=1, tiled=True)
    down_full = lax.all_gather(w_down, TOK, axis=1, tiled=True)

    normed = rms_norm(hidden_states, first_gain)
    length = cached_len[local_req]
    positions = length + block * tok_rows + jnp.arange(tok_rows, dtype=jnp.int32)
    keyval = jnp.dot(normed, w_keyval, preferred_element_type=jnp.float32)
    new_kv = jnp.concatenate(
        [rotate(keyval[:, :kv_cols], positions), keyval[:, kv_cols:]], axis=1
    ).astype(jnp.bfloat16)
    request_kv = gather_rows(new_kv, "rb", lax.axis_size("rb")).reshape(NEW, 2 * kv_cols)
    other_core = 1 - core
    q_wide = jnp.dot(
        lax.dynamic_slice_in_dim(normed, core * half_rows, half_rows, 1),
        wq_mine,
        preferred_element_type=jnp.float32,
    ) + jnp.dot(
        lax.dynamic_slice_in_dim(normed, other_core * half_rows, half_rows, 1),
        wq_other,
        preferred_element_type=jnp.float32,
    )
    queries = rotate(q_wide, positions).astype(jnp.bfloat16)

    local_pages = page_table[local_req] - lax.axis_index(TOK) * kv_cache.shape[0]
    cached = jnp.take(kv_cache, local_pages, axis=0).reshape(MAX_CACHED, 2 * kv_cols)
    grouped_q = (
        queries.reshape(tok_rows, KV_HEADS, group_size, HEAD_DIM)
        .transpose(1, 2, 0, 3)
        .reshape(KV_HEADS, group_size * tok_rows, HEAD_DIM)
    )
    blank = jnp.zeros_like(grouped_q)
    odd = (jnp.arange(KV_HEADS) % 2 == 1)[:, None, None]
    padded_q = jnp.concatenate(
        [jnp.where(odd, blank, grouped_q), jnp.where(odd, grouped_q, blank)], axis=2
    )
    meta = jnp.stack([length, block * tok_rows]).astype(jnp.int32)
    mixed = attend(meta, padded_q, cached, cached, request_kv, request_kv)
    attended = (
        jnp.where(odd, mixed[:, :, HEAD_DIM:], mixed[:, :, :HEAD_DIM])
        .reshape(KV_HEADS, group_size, tok_rows, HEAD_DIM)
        .transpose(2, 0, 1, 3)
        .reshape(tok_rows, HEADS * HEAD_DIM)
    )
    out_mine = jnp.dot(attended, wo_mine, preferred_element_type=jnp.float32)
    out_other = jnp.dot(attended, wo_other, preferred_element_type=jnp.float32)
    first = core == 0
    projected_out = jnp.concatenate(
        [jnp.where(first, out_mine, out_other), jnp.where(first, out_other, out_mine)], axis=1
    )
    middle = (hidden_states.astype(jnp.float32) + projected_out).astype(jnp.bfloat16)
    normed_two = rms_norm(middle, second_gain)

    experts_local = EXPERTS // tp_size
    capacity = 2 * tok_rows * TOP // EXPERTS
    expert_range = jnp.arange(EXPERTS, dtype=jnp.int32)
    onehot = (expert_ids[:, :, None] == expert_range[None, None, :]).astype(jnp.int32)
    per_token = jnp.sum(onehot, axis=1)
    earlier = jnp.cumsum(per_token, axis=0) - per_token
    slot_ids = jnp.sum(onehot * earlier[:, None, :], axis=2)
    target = expert_ids * capacity + slot_ids
    slot_range = jnp.arange(EXPERTS * capacity, dtype=jnp.int32)
    hits = target[None, :, :] == slot_range[:, None, None]
    choose = jnp.any(hits, axis=2).astype(jnp.bfloat16)
    send_buffer = (
        jnp.dot(choose, normed_two, preferred_element_type=jnp.float32)
        .astype(jnp.bfloat16)
        .reshape(tp_size, experts_local, capacity, D)
    )
    returned = []
    for local in range(experts_local):
        received = lax.all_to_all(
            send_buffer[:, local], TP, split_axis=0, concat_axis=0, tiled=True
        ).reshape(tp_size * capacity, D)
        both = jnp.dot(received, gate_up_full[local], preferred_element_type=jnp.float32)
        activated = (jax.nn.silu(both[:, :FF_EXPERT]) * both[:, FF_EXPERT:]).astype(jnp.bfloat16)
        produced = jnp.dot(
            activated, down_full[local], preferred_element_type=jnp.float32
        ).astype(jnp.bfloat16)
        returned.append(
            lax.all_to_all(
                produced.reshape(tp_size, capacity, D), TP, split_axis=0, concat_axis=0, tiled=True
            )
        )
    returned = jnp.stack(returned, axis=1)
    returned = returned.reshape(EXPERTS * capacity, D)
    mixing = jnp.sum(
        jnp.where(hits, gate_weights[None, :, :], 0.0), axis=2
    ).T
    mixture = jnp.dot(
        mixing,
        returned.astype(jnp.float32),
        precision=lax.Precision.HIGHEST,
        preferred_element_type=jnp.float32,
    )
    return (middle.astype(jnp.float32) + mixture).astype(jnp.bfloat16)


def solution(mesh):
    tok_size, tp_size = mesh.devices.shape
    group = tp_size // REQ_DEV
    split = Mesh(mesh.devices.reshape(tok_size // 2, 2, REQ_DEV, group), TOK + TP)
    in_specs = (
        P(TOK + TP, None),
        P(),
        P(),
        P(None, TP),
        P(),
        P(TP, None),
        P(TOK, None, None),
        P(TOK, None),
        P(TOK),
        P(TOK + TP, None),
        P(TOK + TP, None),
        P(TP, TOK, None),
        P(TP, TOK, None),
    )
    out_specs = P(TOK + TP, None)
    return jax.shard_map(shards, mesh=split, in_specs=in_specs, out_specs=out_specs, check_vma=False)
```

```python
import jax
import jax.numpy as jnp
from jax import lax
from jax.experimental import pallas as pl
from jax.experimental.pallas import tpu as pltpu
from jax.sharding import Mesh
from jax.sharding import PartitionSpec as P

D = 1024
HEADS = 16
KV_HEADS = 8
HEAD_DIM = 64
EXPERTS = 32
FF_EXPERT = 512
TOP = 8
NEW = 1024
MAX_CACHED = 2048
REQ_DEV = 2


ATTN_SCALE = 0.015625
EPSILON = 1e-06
THETA = 10000.0

TOK = ("tz", "tc")
TP = ("ra", "rb")


def rms_norm(values, gain):
    wide = values.astype(jnp.float32)
    factor = lax.rsqrt(jnp.mean(wide * wide, axis=-1, keepdims=True) + EPSILON)
    return (wide * factor * gain).astype(jnp.bfloat16)


def rotate(values, positions):
    row_count = values.shape[0]
    shaped = values.reshape(row_count, -1, HEAD_DIM)
    half_dim = HEAD_DIM // 2
    exponent = jnp.arange(half_dim).astype(jnp.float32) * (2.0 / HEAD_DIM)
    frequency = jnp.power(THETA, -exponent)
    angles = positions.astype(jnp.float32)[:, None] * frequency[None, :]
    cosine = jnp.cos(angles)[:, None, :]
    sine_part = jnp.sin(angles)[:, None, :]
    leading = shaped[..., :half_dim]
    trailing = shaped[..., half_dim:]
    turned = jnp.concatenate(
        [leading * cosine - trailing * sine_part, trailing * cosine + leading * sine_part], axis=-1
    )
    return turned.reshape(row_count, -1)


def attention_kernel(meta, q_ref, kc_ref, vc_ref, kn_ref, vn_ref, o_ref):
    length = meta[0]
    first_query = meta[1]
    query = q_ref[0]
    rows = query.shape[0]
    contract = (((1,), (1,)), ((), ()))
    s_old = lax.dot_general(query, kc_ref[...], contract, preferred_element_type=jnp.float32) * ATTN_SCALE
    s_new = lax.dot_general(query, kn_ref[...], contract, preferred_element_type=jnp.float32) * ATTN_SCALE
    old_index = lax.broadcasted_iota(jnp.int32, (1, s_old.shape[1]), 1)
    s_old = jnp.where(old_index < length, s_old, -1e30)
    new_index = lax.broadcasted_iota(jnp.int32, (1, s_new.shape[1]), 1)
    query_index = lax.broadcasted_iota(jnp.int32, (rows, 1), 0) % (rows // 2) + first_query
    s_new = jnp.where(new_index <= query_index, s_new, -1e30)
    top = jnp.maximum(jnp.max(s_old, axis=1, keepdims=True), jnp.max(s_new, axis=1, keepdims=True))
    e_old = jnp.exp(s_old - top)
    e_new = jnp.exp(s_new - top)
    total = jnp.sum(e_old, axis=1, keepdims=True) + jnp.sum(e_new, axis=1, keepdims=True)
    p_old = (e_old / total).astype(jnp.bfloat16)
    p_new = (e_new / total).astype(jnp.bfloat16)
    mixed = jnp.dot(p_old, vc_ref[...], preferred_element_type=jnp.float32) + jnp.dot(
        p_new, vn_ref[...], preferred_element_type=jnp.float32
    )
    o_ref[0] = mixed.astype(o_ref.dtype)


def attend(meta, q, kc, vc, kn, vn):
    groups, rows, _ = q.shape
    old = kc.shape[0]
    new = kn.shape[0]
    lanes = 2 * HEAD_DIM
    values_at = KV_HEADS * HEAD_DIM // lanes
    spec = pl.BlockSpec((1, rows, lanes), lambda c, m: (c, 0, 0))
    keys = lambda n: pl.BlockSpec((n, lanes), lambda c, m: (0, c // 2))
    values = lambda n: pl.BlockSpec((n, lanes), lambda c, m: (0, values_at + c // 2))
    return pl.pallas_call(
        attention_kernel,
        grid_spec=pltpu.PrefetchScalarGridSpec(
            num_scalar_prefetch=1,
            grid=(groups,),
            in_specs=[spec, keys(old), values(old), keys(new), values(new)],
            out_specs=spec,
        ),
        out_shape=jax.ShapeDtypeStruct(q.shape, jnp.bfloat16),
    )(meta, q, kc, vc, kn, vn)


def gather_rows(piece, axis_name, count):
    send = jnp.broadcast_to(piece[None], (count,) + piece.shape)
    return lax.all_to_all(send, axis_name, split_axis=0, concat_axis=0, tiled=True)


def shards(
    hidden_states,
    first_gain,
    second_gain,
    w_query,
    w_keyval,
    w_out,
    kv_cache,
    page_table,
    cached_len,
    expert_ids,
    gate_weights,
    w_gate_up,
    w_down,
):
    tok_rows = hidden_states.shape[0]
    tp_size = lax.axis_size(TP)
    core = lax.axis_index("tc")
    local_req = lax.axis_index("ra")
    block = lax.axis_index("rb")
    kv_cols = KV_HEADS * HEAD_DIM
    group_size = HEADS // KV_HEADS

    half_rows = D // 2
    wq_half = lax.dynamic_slice_in_dim(w_query, core * half_rows, half_rows, 0)
    wo_half = lax.dynamic_slice_in_dim(w_out, core * half_rows, half_rows, 1)
    lanes = 128
    pieces = gather_rows(
        jnp.concatenate([wq_half.reshape(-1, lanes), wo_half.reshape(-1, lanes)], axis=0),
        TP,
        tp_size,
    )
    q_rows = wq_half.size // lanes
    wq_mine = jnp.transpose(
        pieces[:, :q_rows].reshape(tp_size, half_rows, HEAD_DIM), (1, 0, 2)
    ).reshape(half_rows, D)
    wo_mine = pieces[:, q_rows:].reshape(D, half_rows)
    wq_other, wo_other = lax.ppermute((wq_mine, wo_mine), "tc", [(0, 1), (1, 0)])
    gate_up_full = lax.all_gather(w_gate_up, TOK, axis=1, tiled=True)
    down_full = lax.all_gather(w_down, TOK, axis=1, tiled=True)

    normed = rms_norm(hidden_states, first_gain)
    length = cached_len[local_req]
    positions = length + block * tok_rows + jnp.arange(tok_rows, dtype=jnp.int32)
    keyval = jnp.dot(normed, w_keyval, preferred_element_type=jnp.float32)
    new_kv = jnp.concatenate(
        [rotate(keyval[:, :kv_cols], positions), keyval[:, kv_cols:]], axis=1
    ).astype(jnp.bfloat16)
    request_kv = gather_rows(new_kv, "rb", lax.axis_size("rb")).reshape(NEW, 2 * kv_cols)
    other_core = 1 - core
    q_wide = jnp.dot(
        lax.dynamic_slice_in_dim(normed, core * half_rows, half_rows, 1),
        wq_mine,
        preferred_element_type=jnp.float32,
    ) + jnp.dot(
        lax.dynamic_slice_in_dim(normed, other_core * half_rows, half_rows, 1),
        wq_other,
        preferred_element_type=jnp.float32,
    )
    queries = rotate(q_wide, positions).astype(jnp.bfloat16)

    local_pages = page_table[local_req] - lax.axis_index(TOK) * kv_cache.shape[0]
    cached = jnp.take(kv_cache, local_pages, axis=0).reshape(MAX_CACHED, 2 * kv_cols)
    grouped_q = (
        queries.reshape(tok_rows, KV_HEADS, group_size, HEAD_DIM)
        .transpose(1, 2, 0, 3)
        .reshape(KV_HEADS, group_size * tok_rows, HEAD_DIM)
    )
    blank = jnp.zeros_like(grouped_q)
    odd = (jnp.arange(KV_HEADS) % 2 == 1)[:, None, None]
    padded_q = jnp.concatenate(
        [jnp.where(odd, blank, grouped_q), jnp.where(odd, grouped_q, blank)], axis=2
    )
    meta = jnp.stack([length, block * tok_rows]).astype(jnp.int32)
    mixed = attend(meta, padded_q, cached, cached, request_kv, request_kv)
    attended = (
        jnp.where(odd, mixed[:, :, HEAD_DIM:], mixed[:, :, :HEAD_DIM])
        .reshape(KV_HEADS, group_size, tok_rows, HEAD_DIM)
        .transpose(2, 0, 1, 3)
        .reshape(tok_rows, HEADS * HEAD_DIM)
    )
    out_mine = jnp.dot(attended, wo_mine, preferred_element_type=jnp.float32)
    out_other = jnp.dot(attended, wo_other, preferred_element_type=jnp.float32)
    first = core == 0
    projected_out = jnp.concatenate(
        [jnp.where(first, out_mine, out_other), jnp.where(first, out_other, out_mine)], axis=1
    )
    middle = (hidden_states.astype(jnp.float32) + projected_out).astype(jnp.bfloat16)
    normed_two = rms_norm(middle, second_gain)

    experts_local = EXPERTS // tp_size
    capacity = 2 * tok_rows * TOP // EXPERTS
    expert_range = jnp.arange(EXPERTS, dtype=jnp.int32)
    onehot = (expert_ids[:, :, None] == expert_range[None, None, :]).astype(jnp.int32)
    per_token = jnp.sum(onehot, axis=1)
    earlier = jnp.cumsum(per_token, axis=0) - per_token
    slot_ids = jnp.sum(onehot * earlier[:, None, :], axis=2)
    target = expert_ids * capacity + slot_ids
    slot_range = jnp.arange(EXPERTS * capacity, dtype=jnp.int32)
    hits = target[None, :, :] == slot_range[:, None, None]
    choose = jnp.any(hits, axis=2).astype(jnp.bfloat16)
    send_buffer = (
        jnp.dot(choose, normed_two, preferred_element_type=jnp.float32)
        .astype(jnp.bfloat16)
        .reshape(tp_size, experts_local, capacity, D)
    )
    returned = []
    for local in range(experts_local):
        received = lax.all_to_all(
            send_buffer[:, local], TP, split_axis=0, concat_axis=0, tiled=True
        ).reshape(tp_size * capacity, D)
        both = jnp.dot(received, gate_up_full[local], preferred_element_type=jnp.float32)
        activated = (jax.nn.silu(both[:, :FF_EXPERT]) * both[:, FF_EXPERT:]).astype(jnp.bfloat16)
        produced = jnp.dot(
            activated, down_full[local], preferred_element_type=jnp.float32
        ).astype(jnp.bfloat16)
        returned.append(
            lax.all_to_all(
                produced.reshape(tp_size, capacity, D), TP, split_axis=0, concat_axis=0, tiled=True
            )
        )
    returned = jnp.stack(returned, axis=1)
    returned = returned.reshape(EXPERTS * capacity, D)
    mixing = jnp.sum(
        jnp.where(hits, gate_weights[None, :, :], 0.0), axis=2
    ).T
    mixture = jnp.dot(
        mixing,
        returned.astype(jnp.float32),
        precision=lax.Precision.HIGHEST,
        preferred_element_type=jnp.float32,
    )
    return (middle.astype(jnp.float32) + mixture).astype(jnp.bfloat16)


def solution(mesh):
    tok_size, tp_size = mesh.devices.shape
    group = tp_size // REQ_DEV
    split = Mesh(mesh.devices.reshape(tok_size // 2, 2, REQ_DEV, group), TOK + TP)
    in_specs = (
        P(TOK + TP, None),
        P(),
        P(),
        P(None, TP),
        P(),
        P(TP, None),
        P(TOK, None, None),
        P(TOK, None),
        P(TOK),
        P(TOK + TP, None),
        P(TOK + TP, None),
        P(TP, TOK, None),
        P(TP, TOK, None),
    )
    out_specs = P(TOK + TP, None)
    return jax.shard_map(shards, mesh=split, in_specs=in_specs, out_specs=out_specs, check_vma=False)
```

```python
import jax
import jax.numpy as jnp
from jax import lax
from jax.experimental import pallas as pl
from jax.experimental.pallas import tpu as pltpu
from jax.sharding import Mesh
from jax.sharding import PartitionSpec as P

D = 1024
HEADS = 16
KV_HEADS = 8
HEAD_DIM = 64
EXPERTS = 32
FF_EXPERT = 512
TOP = 8
NEW = 1024
MAX_CACHED = 2048
REQ_DEV = 2


ATTN_SCALE = 0.015625
EPSILON = 1e-06
THETA = 10000.0

TOK = ("tz", "tc")
TP = ("ra", "rb")


def rms_norm(values, gain):
    wide = values.astype(jnp.float32)
    factor = lax.rsqrt(jnp.mean(wide * wide, axis=-1, keepdims=True) + EPSILON)
    return (wide * factor * gain).astype(jnp.bfloat16)


def rotate(values, positions):
    row_count = values.shape[0]
    shaped = values.reshape(row_count, -1, HEAD_DIM)
    half_dim = HEAD_DIM // 2
    exponent = jnp.arange(half_dim).astype(jnp.float32) * (2.0 / HEAD_DIM)
    frequency = jnp.power(THETA, -exponent)
    angles = positions.astype(jnp.float32)[:, None] * frequency[None, :]
    cosine = jnp.cos(angles)[:, None, :]
    sine_part = jnp.sin(angles)[:, None, :]
    leading = shaped[..., :half_dim]
    trailing = shaped[..., half_dim:]
    turned = jnp.concatenate(
        [leading * cosine - trailing * sine_part, trailing * cosine + leading * sine_part], axis=-1
    )
    return turned.reshape(row_count, -1)


def attention_kernel(meta, q_ref, kc_ref, vc_ref, kn_ref, vn_ref, o_ref):
    length = meta[0]
    first_query = meta[1]
    query = q_ref[0]
    rows = query.shape[0]
    contract = (((1,), (1,)), ((), ()))
    s_old = lax.dot_general(query, kc_ref[...], contract, preferred_element_type=jnp.float32) * ATTN_SCALE
    s_new = lax.dot_general(query, kn_ref[...], contract, preferred_element_type=jnp.float32) * ATTN_SCALE
    old_index = lax.broadcasted_iota(jnp.int32, (1, s_old.shape[1]), 1)
    s_old = jnp.where(old_index < length, s_old, -1e30)
    new_index = lax.broadcasted_iota(jnp.int32, (1, s_new.shape[1]), 1)
    query_index = lax.broadcasted_iota(jnp.int32, (rows, 1), 0) % (rows // 2) + first_query
    s_new = jnp.where(new_index <= query_index, s_new, -1e30)
    top = jnp.maximum(jnp.max(s_old, axis=1, keepdims=True), jnp.max(s_new, axis=1, keepdims=True))
    e_old = jnp.exp(s_old - top)
    e_new = jnp.exp(s_new - top)
    total = jnp.sum(e_old, axis=1, keepdims=True) + jnp.sum(e_new, axis=1, keepdims=True)
    p_old = (e_old / total).astype(jnp.bfloat16)
    p_new = (e_new / total).astype(jnp.bfloat16)
    mixed = jnp.dot(p_old, vc_ref[...], preferred_element_type=jnp.float32) + jnp.dot(
        p_new, vn_ref[...], preferred_element_type=jnp.float32
    )
    o_ref[0] = mixed.astype(o_ref.dtype)


def attend(meta, q, kc, vc, kn, vn):
    groups, rows, _ = q.shape
    old = kc.shape[0]
    new = kn.shape[0]
    lanes = 2 * HEAD_DIM
    values_at = KV_HEADS * HEAD_DIM // lanes
    spec = pl.BlockSpec((1, rows, lanes), lambda c, m: (c, 0, 0))
    keys = lambda n: pl.BlockSpec((n, lanes), lambda c, m: (0, c // 2))
    values = lambda n: pl.BlockSpec((n, lanes), lambda c, m: (0, values_at + c // 2))
    return pl.pallas_call(
        attention_kernel,
        grid_spec=pltpu.PrefetchScalarGridSpec(
            num_scalar_prefetch=1,
            grid=(groups,),
            in_specs=[spec, keys(old), values(old), keys(new), values(new)],
            out_specs=spec,
        ),
        out_shape=jax.ShapeDtypeStruct(q.shape, jnp.bfloat16),
    )(meta, q, kc, vc, kn, vn)


def gather_rows(piece, axis_name, count):
    send = jnp.broadcast_to(piece[None], (count,) + piece.shape)
    return lax.all_to_all(send, axis_name, split_axis=0, concat_axis=0, tiled=True)


def shards(
    hidden_states,
    first_gain,
    second_gain,
    w_query,
    w_keyval,
    w_out,
    kv_cache,
    page_table,
    cached_len,
    expert_ids,
    gate_weights,
    w_gate_up,
    w_down,
):
    tok_rows = hidden_states.shape[0]
    tp_size = lax.axis_size(TP)
    core = lax.axis_index("tc")
    local_req = lax.axis_index("ra")
    block = lax.axis_index("rb")
    kv_cols = KV_HEADS * HEAD_DIM
    group_size = HEADS // KV_HEADS

    half_rows = D // 2
    wq_half = lax.dynamic_slice_in_dim(w_query, core * half_rows, half_rows, 0)
    wo_half = lax.dynamic_slice_in_dim(w_out, core * half_rows, half_rows, 1)
    lanes = 128
    pieces = gather_rows(
        jnp.concatenate([wq_half.reshape(-1, lanes), wo_half.reshape(-1, lanes)], axis=0),
        TP,
        tp_size,
    )
    q_rows = wq_half.size // lanes
    wq_mine = jnp.transpose(
        pieces[:, :q_rows].reshape(tp_size, half_rows, HEAD_DIM), (1, 0, 2)
    ).reshape(half_rows, D)
    wo_mine = pieces[:, q_rows:].reshape(D, half_rows)
    wq_other, wo_other = lax.ppermute((wq_mine, wo_mine), "tc", [(0, 1), (1, 0)])
    gate_up_full = lax.all_gather(w_gate_up, TOK, axis=1, tiled=True)
    down_full = lax.all_gather(w_down, TOK, axis=1, tiled=True)

    normed = rms_norm(hidden_states, first_gain)
    length = cached_len[local_req]
    positions = length + block * tok_rows + jnp.arange(tok_rows, dtype=jnp.int32)
    keyval = jnp.dot(normed, w_keyval, preferred_element_type=jnp.float32)
    new_kv = jnp.concatenate(
        [rotate(keyval[:, :kv_cols], positions), keyval[:, kv_cols:]], axis=1
    ).astype(jnp.bfloat16)
    request_kv = gather_rows(new_kv, "rb", lax.axis_size("rb")).reshape(NEW, 2 * kv_cols)
    other_core = 1 - core
    q_wide = jnp.dot(
        lax.dynamic_slice_in_dim(normed, core * half_rows, half_rows, 1),
        wq_mine,
        preferred_element_type=jnp.float32,
    ) + jnp.dot(
        lax.dynamic_slice_in_dim(normed, other_core * half_rows, half_rows, 1),
        wq_other,
        preferred_element_type=jnp.float32,
    )
    queries = rotate(q_wide, positions).astype(jnp.bfloat16)

    local_pages = page_table[local_req] - lax.axis_index(TOK) * kv_cache.shape[0]
    cached = jnp.take(kv_cache, local_pages, axis=0).reshape(MAX_CACHED, 2 * kv_cols)
    grouped_q = (
        queries.reshape(tok_rows, KV_HEADS, group_size, HEAD_DIM)
        .transpose(1, 2, 0, 3)
        .reshape(KV_HEADS, group_size * tok_rows, HEAD_DIM)
    )
    blank = jnp.zeros_like(grouped_q)
    odd = (jnp.arange(KV_HEADS) % 2 == 1)[:, None, None]
    padded_q = jnp.concatenate(
        [jnp.where(odd, blank, grouped_q), jnp.where(odd, grouped_q, blank)], axis=2
    )
    meta = jnp.stack([length, block * tok_rows]).astype(jnp.int32)
    mixed = attend(meta, padded_q, cached, cached, request_kv, request_kv)
    attended = (
        jnp.where(odd, mixed[:, :, HEAD_DIM:], mixed[:, :, :HEAD_DIM])
        .reshape(KV_HEADS, group_size, tok_rows, HEAD_DIM)
        .transpose(2, 0, 1, 3)
        .reshape(tok_rows, HEADS * HEAD_DIM)
    )
    out_mine = jnp.dot(attended, wo_mine, preferred_element_type=jnp.float32)
    out_other = jnp.dot(attended, wo_other, preferred_element_type=jnp.float32)
    first = core == 0
    projected_out = jnp.concatenate(
        [jnp.where(first, out_mine, out_other), jnp.where(first, out_other, out_mine)], axis=1
    )
    middle = (hidden_states.astype(jnp.float32) + projected_out).astype(jnp.bfloat16)
    normed_two = rms_norm(middle, second_gain)

    experts_local = EXPERTS // tp_size
    capacity = 2 * tok_rows * TOP // EXPERTS
    expert_range = jnp.arange(EXPERTS, dtype=jnp.int32)
    onehot = (expert_ids[:, :, None] == expert_range[None, None, :]).astype(jnp.int32)
    per_token = jnp.sum(onehot, axis=1)
    earlier = jnp.cumsum(per_token, axis=0) - per_token
    slot_ids = jnp.sum(onehot * earlier[:, None, :], axis=2)
    target = expert_ids * capacity + slot_ids
    slot_range = jnp.arange(EXPERTS * capacity, dtype=jnp.int32)
    hits = target[None, :, :] == slot_range[:, None, None]
    choose = jnp.any(hits, axis=2).astype(jnp.bfloat16)
    send_buffer = (
        jnp.dot(choose, normed_two, preferred_element_type=jnp.float32)
        .astype(jnp.bfloat16)
        .reshape(tp_size, experts_local, capacity, D)
    )
    returned = []
    for local in range(experts_local):
        received = lax.all_to_all(
            send_buffer[:, local], TP, split_axis=0, concat_axis=0, tiled=True
        ).reshape(tp_size * capacity, D)
        both = jnp.dot(received, gate_up_full[local], preferred_element_type=jnp.float32)
        activated = (jax.nn.silu(both[:, :FF_EXPERT]) * both[:, FF_EXPERT:]).astype(jnp.bfloat16)
        produced = jnp.dot(
            activated, down_full[local], preferred_element_type=jnp.float32
        ).astype(jnp.bfloat16)
        returned.append(
            lax.all_to_all(
                produced.reshape(tp_size, capacity, D), TP, split_axis=0, concat_axis=0, tiled=True
            )
        )
    mixing = jnp.sum(jnp.where(hits, gate_weights[None, :, :], 0.0), axis=2).T.reshape(
        tok_rows, tp_size, experts_local, capacity
    )
    mixture = sum(
        jnp.dot(
            mixing[:, :, local].reshape(tok_rows, tp_size * capacity),
            returned[local].reshape(tp_size * capacity, D).astype(jnp.float32),
            precision=lax.Precision.HIGHEST,
            preferred_element_type=jnp.float32,
        )
        for local in range(experts_local)
    )
    return (middle.astype(jnp.float32) + mixture).astype(jnp.bfloat16)


def solution(mesh):
    tok_size, tp_size = mesh.devices.shape
    group = tp_size // REQ_DEV
    split = Mesh(mesh.devices.reshape(tok_size // 2, 2, REQ_DEV, group), TOK + TP)
    in_specs = (
        P(TOK + TP, None),
        P(),
        P(),
        P(None, TP),
        P(),
        P(TP, None),
        P(TOK, None, None),
        P(TOK, None),
        P(TOK),
        P(TOK + TP, None),
        P(TOK + TP, None),
        P(TP, TOK, None),
        P(TP, TOK, None),
    )
    out_specs = P(TOK + TP, None)
    return jax.shard_map(shards, mesh=split, in_specs=in_specs, out_specs=out_specs, check_vma=False)
```
